32 devices in a mesh: groups: 2 (over y), context: 4 (over x, core), tensor: 4 (over z).
Axes of the slice: x: 2, y: 2, z: 4, core: 2. Of those that a mesh axis runs over, the one named last changes fastest.
Arguments:
- tokens: bfloat16 [8192, 1920], P(('groups', 'context'), 'tensor'), parts along dimension 0, may hold values from -6 to 6
- in_weight: bfloat16 [1920, 3, 1920], P(None, None, 'tensor'), may hold values from -0.125 to 0.125
- short_filter: bfloat16 [7, 3, 1920], P(None, None, 'tensor'), may hold values from -2 to 2
- mode_weight: float32 [1920, 16], P('tensor'), may hold values from -1.5 to 1.5
- decay_rate: float32 [1920, 16], P('tensor'), as said below
- out_weight: bfloat16 [1920, 1920], P('tensor'), may hold values from -0.1875 to 0.1875
Outputs:
- mixed: bfloat16 [8192, 1920], P(('groups', 'context'), 'tensor'), parts along dimension 0
The draws below stay inside these ranges and needn't reach their ends.
There are 2 independent parts, one for each index of `groups`. The reference program is written for one: setup_inputs(seed, part) draws one part's arguments, and reference() takes and returns one part's arrays. A program takes and returns all parts, laid end to end along the dimension named above; an argument that names none is the same for every part. Nothing has to cross between parts.
Inputs may be any that keep to these rules, and one draw needn't show every extreme that they name: `decay_rate`: every rate lies between 0.2 / 4096 and 1 / 30.
All inputs are finite; a program needn't handle non-finite values.
Results may differ from the reference program's by a relative error of at most 0.025.
Values may be sent and summed in bfloat16 or wider, within the bound.
No kernel may reach another device: no remote copies, remote signals or barrier semaphores. Data moves between devices by JAX's collectives and lax.ppermute only.
A program may use at most 64 MiB of HBM per device.

```python
import jax
import jax.numpy as jnp
from jax import lax

D = 1920
MODES = 16
TAPS = 7
L = 4096
N_TENSOR = 4


def draw_decay_rate(key, part):
    first, second, third = jax.random.split(key, 3)
    share = 0.5
    slow_pick = jax.random.uniform(first, (D, MODES), jnp.float32) < share
    slow_log = jax.random.uniform(second, (D, MODES), jnp.float32, jnp.log(0.2 / L), jnp.log(2.0 / L))
    fast_log = jax.random.uniform(third, (D, MODES), jnp.float32, jnp.log(2.0 / L), jnp.log(1.0 / 30.0))
    return jnp.exp(jnp.where(slow_pick, slow_log, fast_log)).astype(jnp.float32)


def with_spikes(result, own_key, source, target, shards_of, factor):
    def block_of(dim):
        return (jnp.arange(result.shape[dim]) // (result.shape[dim] // shards_of)).reshape((-1,) + (1,) * (result.ndim - 1 - dim))

    near = jax.random.permutation(own_key, shards_of)[block_of(target)]
    other_side = (block_of(target) + shards_of // 2) % shards_of
    return jnp.where((block_of(source) == near) | (block_of(source) == other_side), factor * result, result)


def steps_of(stream_key, shape, cuts, least, largest):
    def one(axis_at, parts):
        draws = jax.random.uniform(jax.random.fold_in(jax.random.fold_in(stream_key, 6), axis_at), (parts,), jnp.float32, least / len(cuts), largest / len(cuts))
        return jnp.repeat(jnp.exp(draws), shape[axis_at] // parts).reshape((-1,) + (1,) * (len(shape) - axis_at - 1))

    level = one(*cuts[0])
    for cut in cuts[1:]:
        level = level * one(*cut)
    return level


def gaussian(stream_key, dims, scale, reach, pieces=(), held_as=jnp.bfloat16):
    entries = jax.random.normal(stream_key, dims, jnp.float32) * scale
    if len(pieces) > 0:
        entries = steps_of(stream_key, dims, pieces, -0.22, 0.18) * entries
    return jnp.clip(entries, min=-reach, max=reach).astype(held_as)


def gaussian_with(own_key, extent, deviation, reach, shards, heavy, kind=jnp.bfloat16):
    values = deviation * jax.random.normal(own_key, extent, jnp.float32)
    if shards:
        values = values * steps_of(own_key, extent, shards, -0.22, 0.18)
    return jnp.clip(with_spikes(values, jax.random.fold_in(own_key, 3), *heavy), -reach, reach).astype(kind)


def setup_inputs(seed: int = 0, part: int = 0) -> dict:
    streams_of = jax.random.split(jax.random.key(seed), 7)
    own_keys = jax.random.split(jax.random.fold_in(streams_of[6], part), 7)
    return {
        "tokens": gaussian(own_keys[0], (L, D), 1.0, 6.0, ((0, 4), (1, 4))),
        "in_weight": gaussian(streams_of[1], (D, 3, D), D ** -0.5, 0.125, ((2, 4),)),
        "short_filter": gaussian(streams_of[2], (TAPS, 3, D), 0.4, 2.0, ((2, 4),)),
        "mode_weight": gaussian(streams_of[3], (D, MODES), MODES ** -0.5, 1.5, ((0, 4),), jnp.float32),
        "decay_rate": draw_decay_rate(jax.random.fold_in(streams_of[6], 71), part),
        "out_weight": gaussian_with(streams_of[5], (D, D), D ** -0.5, 0.1875, ((0, 4),), (0, 1, 4, 2.0)),
    }


def reference(tokens, in_weight, short_filter, mode_weight, decay_rate, out_weight):
    proj = jnp.dot(tokens, in_weight.reshape(D, 3 * D), preferred_element_type=jnp.float32)
    proj = proj.reshape(L, 3, D).astype(jnp.bfloat16)
    padded = jnp.concatenate([jnp.zeros((TAPS - 1, 3, D), jnp.bfloat16), proj], 0)
    filtered = jnp.zeros((L, 3, D), jnp.float32)
    for tap_number in range(TAPS):
        begin = TAPS - 1 - tap_number
        filtered = filtered + short_filter[tap_number].astype(jnp.float32)[None] * padded[begin:begin + L].astype(jnp.float32)
    query = filtered[:, 0]
    drive = filtered[:, 1] * filtered[:, 2]
    lags = jnp.arange(L).astype(jnp.float32)
    amplitude = mode_weight * jnp.sqrt(2.0 * decay_rate)
    kernel = jnp.zeros((L, D), jnp.float32)
    for mode_number in range(MODES):
        kernel = kernel + amplitude[:, mode_number][None, :] * jnp.exp(-decay_rate[:, mode_number][None, :] * lags[:, None])
    spectrum = jnp.fft.rfft(drive, n=2 * L, axis=0) * jnp.fft.rfft(kernel, n=2 * L, axis=0)
    conv = jnp.fft.irfft(spectrum, n=2 * L, axis=0)[:L].astype(jnp.float32)
    gated = (query * conv).astype(jnp.bfloat16)
    width = D // N_TENSOR
    total = jnp.zeros((L, D), jnp.float32)
    for group_number in range(N_TENSOR):
        partial_sum = jnp.dot(gated[:, group_number * width:(group_number + 1) * width], out_weight[group_number * width:(group_number + 1) * width], preferred_element_type=jnp.float32).astype(jnp.bfloat16)
        partial_sum = lax.optimization_barrier(partial_sum)
        total = total + partial_sum.astype(jnp.float32)
    return total.astype(jnp.bfloat16)
```

```python
import jax
import jax.numpy as jnp
from jax import lax
from jax.experimental import pallas as pl
from jax.experimental.pallas import tpu as pltpu
from jax.sharding import PartitionSpec as P

TAPS = 7
CHUNK = 8


def shifted(array, axis, by):
    size = lax.axis_size(axis)
    pairs = [(i, i + by) for i in range(size) if 0 <= i + by < size]
    return lax.ppermute(array, axis, pairs)


def local_kernel(d_ref, hcol_ref, w_ref, g_ref, a8_ref, conv_ref, end_ref, s_ref):
    rows = d_ref.shape[0]
    modes = a8_ref.shape[0]
    s_ref[...] = jnp.zeros(s_ref.shape, jnp.float32)

    def body(b, carry):
        start = pl.multiple_of(b * CHUNK, CHUNK)
        state = s_ref[...]
        chunk = d_ref[pl.ds(start, CHUNK), :]
        acc = jnp.zeros(chunk.shape, jnp.float32)
        for n in range(modes):
            acc = acc + g_ref[n] * state[n : n + 1, :]
        new_state = a8_ref[...] * state
        for j in range(CHUNK):
            row = chunk[j : j + 1, :]
            acc = acc + hcol_ref[j] * row
            new_state = new_state + w_ref[j] * row
        conv_ref[pl.ds(start, CHUNK), :] = acc
        s_ref[...] = new_state
        return carry

    lax.fori_loop(0, rows // CHUNK, body, 0)
    end_ref[...] = s_ref[...]


def gate_kernel(conv_ref, q_ref, g_ref, a8_ref, sin_ref, out_ref, s_ref):
    rows = conv_ref.shape[0]
    modes = a8_ref.shape[0]
    s_ref[...] = sin_ref[...]

    def body(b, carry):
        start = pl.multiple_of(b * CHUNK, CHUNK)
        state = s_ref[...]
        acc = conv_ref[pl.ds(start, CHUNK), :]
        for n in range(modes):
            acc = acc + g_ref[n] * state[n : n + 1, :]
        out_ref[pl.ds(start, CHUNK), :] = q_ref[pl.ds(start, CHUNK), :] * acc
        s_ref[...] = a8_ref[...] * state
        return carry

    lax.fori_loop(0, rows // CHUNK, body, 0)


def vmem_spec():
    return pl.BlockSpec(memory_space=pltpu.VMEM)


def per_device(tokens, in_weight, short_filter, mode_weight, decay_rate, out_weight):
    tok_rows = tokens.shape[0]
    channels = in_weight.shape[2]
    modes = decay_rate.shape[1]
    proj = jnp.einsum(
        "td,dkc->tkc",
        lax.all_gather(tokens, "tensor", axis=1, tiled=True),
        in_weight,
        preferred_element_type=jnp.float32,
    ).astype(jnp.bfloat16)
    rim = shifted(proj[tok_rows - (TAPS - 1) :], "context", 1)
    padded = jnp.concatenate([rim, proj], 0)
    filtered = jnp.zeros((tok_rows, 3, channels), jnp.float32)
    for tap_number in range(TAPS):
        begin = TAPS - 1 - tap_number
        filtered = filtered + short_filter[tap_number].astype(jnp.float32)[None] * padded[
            begin : begin + tok_rows
        ].astype(jnp.float32)
    query = filtered[:, 0]
    drive = filtered[:, 1] * filtered[:, 2]

    lam = decay_rate.T
    amp = (mode_weight * jnp.sqrt(2.0 * decay_rate)).T
    steps = jnp.arange(CHUNK).astype(jnp.float32)
    g_tab = amp[:, None, :] * jnp.exp(-lam[:, None, :] * steps[None, :, None])
    w_tab = jnp.exp(-lam[None, :, :] * (CHUNK - steps)[:, None, None])
    h_short = jnp.sum(g_tab, axis=0)
    lag = steps[None, :] - steps[:, None]
    lag_index = jnp.clip(lag, 0, CHUNK - 1).astype(jnp.int32)
    hcol = jnp.where((lag >= 0)[:, :, None], h_short[lag_index], 0.0)
    a8 = jnp.exp(-lam * CHUNK)

    conv_local, end_state = pl.pallas_call(
        local_kernel,
        out_shape=(
            jax.ShapeDtypeStruct((tok_rows, channels), jnp.float32),
            jax.ShapeDtypeStruct((modes, channels), jnp.float32),
        ),
        in_specs=[vmem_spec() for _ in range(5)],
        out_specs=(vmem_spec(), vmem_spec()),
        scratch_shapes=[pltpu.VMEM((modes, channels), jnp.float32)],
    )(drive, hcol, w_tab, g_tab, a8)

    ends = lax.all_gather(end_state, "context", axis=0, tiled=False)
    block_count = ends.shape[0]
    me = lax.axis_index("context")
    gap = (me - 1 - jnp.arange(block_count)).astype(jnp.float32)
    factor = jnp.where(
        (gap >= 0.0)[:, None, None],
        jnp.exp(-lam[None] * (tok_rows * jnp.maximum(gap, 0.0))[:, None, None]),
        0.0,
    )
    state_in = jnp.sum(factor * ends, axis=0)

    gated = pl.pallas_call(
        gate_kernel,
        out_shape=jax.ShapeDtypeStruct((tok_rows, channels), jnp.float32),
        in_specs=[vmem_spec() for _ in range(5)],
        out_specs=vmem_spec(),
        scratch_shapes=[pltpu.VMEM((modes, channels), jnp.float32)],
    )(conv_local, query, g_tab, a8, state_in)
    gated = gated.astype(jnp.bfloat16)
    partial_sums = jnp.dot(gated, out_weight, preferred_element_type=jnp.float32)
    summed = lax.psum_scatter(
        partial_sums.astype(jnp.bfloat16), "tensor", scatter_dimension=1, tiled=True
    )
    return summed


def solution(mesh):
    placed = (
        P(("groups", "context"), "tensor"),
        P(None, None, "tensor"),
        P(None, None, "tensor"),
        P("tensor", None),
        P("tensor", None),
        P("tensor", None),
    )
    return jax.shard_map(
        per_device,
        mesh=mesh,
        in_specs=placed,
        out_specs=P(("groups", "context"), "tensor"),
        check_vma=False,
    )
```

```python
import jax
import jax.numpy as jnp
from jax import lax
from jax.experimental import pallas as pl
from jax.experimental.pallas import tpu as pltpu
from jax.sharding import PartitionSpec as P

TAPS = 7
CHUNK = 8


def shifted(array, axis, by):
    size = lax.axis_size(axis)
    pairs = [(i, i + by) for i in range(size) if 0 <= i + by < size]
    return lax.ppermute(array, axis, pairs)


def local_kernel(d_ref, hcol_ref, w_ref, g_ref, a8_ref, conv_ref, end_ref, s_ref):
    rows = d_ref.shape[0]
    modes = a8_ref.shape[0]
    s_ref[...] = jnp.zeros(s_ref.shape, jnp.float32)

    def body(b, carry):
        start = pl.multiple_of(b * CHUNK, CHUNK)
        state = s_ref[...]
        chunk = d_ref[pl.ds(start, CHUNK), :]
        acc = jnp.zeros(chunk.shape, jnp.float32)
        for n in range(modes):
            acc = acc + g_ref[n] * state[n : n + 1, :]
        new_state = a8_ref[...] * state
        for j in range(CHUNK):
            row = chunk[j : j + 1, :]
            acc = acc + hcol_ref[j] * row
            new_state = new_state + w_ref[j] * row
        conv_ref[pl.ds(start, CHUNK), :] = acc
        s_ref[...] = new_state
        return carry

    lax.fori_loop(0, rows // CHUNK, body, 0)
    end_ref[...] = s_ref[...]


def gate_kernel(conv_ref, q_ref, g_ref, a8_ref, sin_ref, out_ref, s_ref):
    rows = conv_ref.shape[0]
    modes = a8_ref.shape[0]
    s_ref[...] = sin_ref[...]

    def body(b, carry):
        start = pl.multiple_of(b * CHUNK, CHUNK)
        state = s_ref[...]
        acc = conv_ref[pl.ds(start, CHUNK), :]
        for n in range(modes):
            acc = acc + g_ref[n] * state[n : n + 1, :]
        out_ref[pl.ds(start, CHUNK), :] = q_ref[pl.ds(start, CHUNK), :] * acc
        s_ref[...] = a8_ref[...] * state
        return carry

    lax.fori_loop(0, rows // CHUNK, body, 0)


def vmem_spec():
    return pl.BlockSpec(memory_space=pltpu.VMEM)


NCH = 2


def chunk_tables(decay_rate, mode_weight):
    lam = decay_rate.T
    amp = (mode_weight * jnp.sqrt(2.0 * decay_rate)).T
    steps = jnp.arange(CHUNK).astype(jnp.float32)
    g_tab = amp[:, None, :] * jnp.exp(-lam[:, None, :] * steps[None, :, None])
    w_tab = jnp.exp(-lam[None, :, :] * (CHUNK - steps)[:, None, None])
    h_short = jnp.sum(g_tab, axis=0)
    lag = steps[None, :] - steps[:, None]
    lag_index = jnp.clip(lag, 0, CHUNK - 1).astype(jnp.int32)
    hcol = jnp.where((lag >= 0)[:, :, None], h_short[lag_index], 0.0)
    a8 = jnp.exp(-lam * CHUNK)
    return lam, g_tab, w_tab, hcol, a8


def local_conv(drive, hcol, w_tab, g_tab, a8):
    rows, channels = drive.shape
    modes = a8.shape[0]
    return pl.pallas_call(
        local_kernel,
        out_shape=(
            jax.ShapeDtypeStruct((rows, channels), jnp.float32),
            jax.ShapeDtypeStruct((modes, channels), jnp.float32),
        ),
        in_specs=[vmem_spec() for _ in range(5)],
        out_specs=(vmem_spec(), vmem_spec()),
        scratch_shapes=[pltpu.VMEM((modes, channels), jnp.float32)],
    )(drive, hcol, w_tab, g_tab, a8)


def gate(conv_local, query, g_tab, a8, state_in):
    rows, channels = conv_local.shape
    modes = a8.shape[0]
    return pl.pallas_call(
        gate_kernel,
        out_shape=jax.ShapeDtypeStruct((rows, channels), jnp.float32),
        in_specs=[vmem_spec() for _ in range(5)],
        out_specs=vmem_spec(),
        scratch_shapes=[pltpu.VMEM((modes, channels), jnp.float32)],
    )(conv_local, query, g_tab, a8, state_in)


def per_device(tokens, in_weight, short_filter, mode_weight, decay_rate, out_weight):
    tok_rows = tokens.shape[0]
    channels = in_weight.shape[2]
    rim_rows = TAPS - 1
    piece = tok_rows // NCH
    lam, g_tab, w_tab, hcol, a8 = chunk_tables(decay_rate, mode_weight)
    taps = short_filter.astype(jnp.float32)

    rim = shifted(tokens[tok_rows - rim_rows :], "context", 1)
    queries, convs, ends = [], [], []
    for k in range(NCH):
        before = rim if k == 0 else tokens[k * piece - rim_rows : k * piece]
        ext = jnp.concatenate([before, tokens[k * piece : (k + 1) * piece]], 0)
        full = lax.all_gather(ext, "tensor", axis=1, tiled=True)
        proj = jnp.einsum(
            "td,dkc->tkc", full, in_weight, preferred_element_type=jnp.float32
        ).astype(jnp.bfloat16)
        filtered = jnp.zeros((piece, 3, channels), jnp.float32)
        for tap_number in range(TAPS):
            begin = rim_rows - tap_number
            filtered = filtered + taps[tap_number][None] * proj[begin : begin + piece].astype(
                jnp.float32
            )
        drive = filtered[:, 1] * filtered[:, 2]
        conv_local, end_state = local_conv(drive, hcol, w_tab, g_tab, a8)
        queries.append(filtered[:, 0])
        convs.append(conv_local)
        ends.append(end_state)

    piece_decay = jnp.exp(-lam * piece)
    block_end = jnp.zeros_like(ends[0])
    for k in range(NCH):
        block_end = piece_decay * block_end + ends[k]
    state_in = jnp.zeros_like(block_end)
    for by in range(1, lax.axis_size("context")):
        earlier = shifted(block_end, "context", by)
        state_in = state_in + jnp.exp(-lam * (tok_rows * (by - 1))) * earlier

    outs = []
    state = state_in
    for k in range(NCH):
        gated = gate(convs[k], queries[k], g_tab, a8, state).astype(jnp.bfloat16)
        state = piece_decay * state + ends[k]
        partial_sums = jnp.dot(gated, out_weight, preferred_element_type=jnp.float32)
        outs.append(
            lax.psum_scatter(
                partial_sums.astype(jnp.bfloat16), "tensor", scatter_dimension=1, tiled=True
            )
        )
    return jnp.concatenate(outs, 0)


def solution(mesh):
    placed = (
        P(("groups", "context"), "tensor"),
        P(None, None, "tensor"),
        P(None, None, "tensor"),
        P("tensor", None),
        P("tensor", None),
        P("tensor", None),
    )
    return jax.shard_map(
        per_device,
        mesh=mesh,
        in_specs=placed,
        out_specs=P(("groups", "context"), "tensor"),
        check_vma=False,
    )
```

```python
import jax
import jax.numpy as jnp
from jax import lax
from jax.experimental import pallas as pl
from jax.experimental.pallas import tpu as pltpu
from jax.sharding import PartitionSpec as P

TAPS = 7
CHUNK = 8


def shifted(array, axis, by):
    size = lax.axis_size(axis)
    pairs = [(i, i + by) for i in range(size) if 0 <= i + by < size]
    return lax.ppermute(array, axis, pairs)


def local_kernel(d_ref, hcol_ref, w_ref, g_ref, a8_ref, conv_ref, end_ref, s_ref):
    rows = d_ref.shape[0]
    modes = a8_ref.shape[0]
    s_ref[...] = jnp.zeros(s_ref.shape, jnp.float32)

    def body(b, carry):
        start = pl.multiple_of(b * CHUNK, CHUNK)
        state = s_ref[...]
        chunk = d_ref[pl.ds(start, CHUNK), :]
        acc = jnp.zeros(chunk.shape, jnp.float32)
        for n in range(modes):
            acc = acc + g_ref[n] * state[n : n + 1, :]
        new_state = a8_ref[...] * state
        for j in range(CHUNK):
            row = chunk[j : j + 1, :]
            acc = acc + hcol_ref[j] * row
            new_state = new_state + w_ref[j] * row
        conv_ref[pl.ds(start, CHUNK), :] = acc
        s_ref[...] = new_state
        return carry

    lax.fori_loop(0, rows // CHUNK, body, 0)
    end_ref[...] = s_ref[...]


def gate_kernel(conv_ref, q_ref, g_ref, a8_ref, sin_ref, out_ref, s_ref):
    rows = conv_ref.shape[0]
    modes = a8_ref.shape[0]
    s_ref[...] = sin_ref[...]

    def body(b, carry):
        start = pl.multiple_of(b * CHUNK, CHUNK)
        state = s_ref[...]
        acc = conv_ref[pl.ds(start, CHUNK), :]
        for n in range(modes):
            acc = acc + g_ref[n] * state[n : n + 1, :]
        out_ref[pl.ds(start, CHUNK), :] = q_ref[pl.ds(start, CHUNK), :] * acc
        s_ref[...] = a8_ref[...] * state
        return carry

    lax.fori_loop(0, rows // CHUNK, body, 0)


def vmem_spec():
    return pl.BlockSpec(memory_space=pltpu.VMEM)


def chunk_tables(decay_rate, mode_weight):
    lam = decay_rate.T
    amp = (mode_weight * jnp.sqrt(2.0 * decay_rate)).T
    steps = jnp.arange(CHUNK).astype(jnp.float32)
    g_tab = amp[:, None, :] * jnp.exp(-lam[:, None, :] * steps[None, :, None])
    w_tab = jnp.exp(-lam[None, :, :] * (CHUNK - steps)[:, None, None])
    h_short = jnp.sum(g_tab, axis=0)
    lag = steps[None, :] - steps[:, None]
    lag_index = jnp.clip(lag, 0, CHUNK - 1).astype(jnp.int32)
    hcol = jnp.where((lag >= 0)[:, :, None], h_short[lag_index], 0.0)
    a8 = jnp.exp(-lam * CHUNK)
    return lam, g_tab, w_tab, hcol, a8


def local_conv(drive, hcol, w_tab, g_tab, a8):
    rows, channels = drive.shape
    modes = a8.shape[0]
    return pl.pallas_call(
        local_kernel,
        out_shape=(
            jax.ShapeDtypeStruct((rows, channels), jnp.float32),
            jax.ShapeDtypeStruct((modes, channels), jnp.float32),
        ),
        in_specs=[vmem_spec() for _ in range(5)],
        out_specs=(vmem_spec(), vmem_spec()),
        scratch_shapes=[pltpu.VMEM((modes, channels), jnp.float32)],
    )(drive, hcol, w_tab, g_tab, a8)


def gate(conv_local, query, g_tab, a8, state_in):
    rows, channels = conv_local.shape
    modes = a8.shape[0]
    return pl.pallas_call(
        gate_kernel,
        out_shape=jax.ShapeDtypeStruct((rows, channels), jnp.float32),
        in_specs=[vmem_spec() for _ in range(5)],
        out_specs=vmem_spec(),
        scratch_shapes=[pltpu.VMEM((modes, channels), jnp.float32)],
    )(conv_local, query, g_tab, a8, state_in)


def relay_pairs(size, step, forward):
    if forward:
        return [(i, i + 1) for i in range(step - 1, size - 1)]
    return [(i, i - 1) for i in range(1, size - step + 1)]


def gathered_projection(tokens, in_weight):
    size = lax.axis_size("tensor")
    me = lax.axis_index("tensor")
    feats = tokens.shape[1]

    def rows_of(owner):
        owner = jnp.clip(owner, 0, size - 1)
        return lax.dynamic_slice_in_dim(in_weight, owner * feats, feats, 0)

    acc = jnp.einsum("td,dkc->tkc", tokens, rows_of(me), preferred_element_type=jnp.float32)
    fwd = tokens
    bwd = tokens
    for step in range(1, size):
        fwd = lax.ppermute(fwd, "tensor", relay_pairs(size, step, True))
        bwd = lax.ppermute(bwd, "tensor", relay_pairs(size, step, False))
        acc = acc + jnp.einsum(
            "td,dkc->tkc", fwd, rows_of(me - step), preferred_element_type=jnp.float32
        )
        acc = acc + jnp.einsum(
            "td,dkc->tkc", bwd, rows_of(me + step), preferred_element_type=jnp.float32
        )
    return acc.astype(jnp.bfloat16)


def per_device(tokens, in_weight, short_filter, mode_weight, decay_rate, out_weight):
    tok_rows = tokens.shape[0]
    channels = in_weight.shape[2]
    rim_rows = TAPS - 1
    lam, g_tab, w_tab, hcol, a8 = chunk_tables(decay_rate, mode_weight)
    taps = short_filter.astype(jnp.float32)

    proj = gathered_projection(tokens, in_weight)
    rim = shifted(proj[tok_rows - rim_rows :], "context", 1)
    padded = jnp.concatenate([rim, proj], 0)
    filtered = jnp.zeros((tok_rows, 3, channels), jnp.float32)
    for tap_number in range(TAPS):
        begin = rim_rows - tap_number
        filtered = filtered + taps[tap_number][None] * padded[begin : begin + tok_rows].astype(
            jnp.float32
        )
    query = filtered[:, 0]
    drive = filtered[:, 1] * filtered[:, 2]
    conv_local, block_end = local_conv(drive, hcol, w_tab, g_tab, a8)

    state_in = jnp.zeros_like(block_end)
    for by in range(1, lax.axis_size("context")):
        earlier = shifted(block_end, "context", by)
        state_in = state_in + jnp.exp(-lam * (tok_rows * (by - 1))) * earlier

    gated = gate(conv_local, query, g_tab, a8, state_in).astype(jnp.bfloat16)
    partial_sums = jnp.dot(gated, out_weight, preferred_element_type=jnp.float32)
    return lax.psum_scatter(
        partial_sums.astype(jnp.bfloat16), "tensor", scatter_dimension=1, tiled=True
    )


def solution(mesh):
    placed = (
        P(("groups", "context"), "tensor"),
        P(None, None, "tensor"),
        P(None, None, "tensor"),
        P("tensor", None),
        P("tensor", None),
        P("tensor", None),
    )
    return jax.shard_map(
        per_device,
        mesh=mesh,
        in_specs=placed,
        out_specs=P(("groups", "context"), "tensor"),
        check_vma=False,
    )
```

```python
import jax
import jax.numpy as jnp
from jax import lax
from jax.experimental import pallas as pl
from jax.experimental.pallas import tpu as pltpu
from jax.sharding import PartitionSpec as P

TAPS = 7
CHUNK = 8


def shifted(array, axis, by):
    size = lax.axis_size(axis)
    pairs = [(i, i + by) for i in range(size) if 0 <= i + by < size]
    return lax.ppermute(array, axis, pairs)


def local_kernel(d_ref, hcol_ref, w_ref, g_ref, a8_ref, conv_ref, end_ref, s_ref):
    rows = d_ref.shape[0]
    modes = a8_ref.shape[0]
    s_ref[...] = jnp.zeros(s_ref.shape, jnp.float32)

    def body(b, carry):
        start = pl.multiple_of(b * CHUNK, CHUNK)
        state = s_ref[...]
        chunk = d_ref[pl.ds(start, CHUNK), :]
        acc = jnp.zeros(chunk.shape, jnp.float32)
        for n in range(modes):
            acc = acc + g_ref[n] * state[n : n + 1, :]
        new_state = a8_ref[...] * state
        for j in range(CHUNK):
            row = chunk[j : j + 1, :]
            acc = acc + hcol_ref[j] * row
            new_state = new_state + w_ref[j] * row
        conv_ref[pl.ds(start, CHUNK), :] = acc
        s_ref[...] = new_state
        return carry

    lax.fori_loop(0, rows // CHUNK, body, 0)
    end_ref[...] = s_ref[...]


def gate_kernel(conv_ref, q_ref, g_ref, a8_ref, sin_ref, out_ref, s_ref):
    rows = conv_ref.shape[0]
    modes = a8_ref.shape[0]
    s_ref[...] = sin_ref[...]

    def body(b, carry):
        start = pl.multiple_of(b * CHUNK, CHUNK)
        state = s_ref[...]
        acc = conv_ref[pl.ds(start, CHUNK), :]
        for n in range(modes):
            acc = acc + g_ref[n] * state[n : n + 1, :]
        out_ref[pl.ds(start, CHUNK), :] = q_ref[pl.ds(start, CHUNK), :] * acc
        s_ref[...] = a8_ref[...] * state
        return carry

    lax.fori_loop(0, rows // CHUNK, body, 0)


def vmem_spec():
    return pl.BlockSpec(memory_space=pltpu.VMEM)


def chunk_tables(decay_rate, mode_weight):
    lam = decay_rate.T
    amp = (mode_weight * jnp.sqrt(2.0 * decay_rate)).T
    steps = jnp.arange(CHUNK).astype(jnp.float32)
    g_tab = amp[:, None, :] * jnp.exp(-lam[:, None, :] * steps[None, :, None])
    w_tab = jnp.exp(-lam[None, :, :] * (CHUNK - steps)[:, None, None])
    h_short = jnp.sum(g_tab, axis=0)
    lag = steps[None, :] - steps[:, None]
    lag_index = jnp.clip(lag, 0, CHUNK - 1).astype(jnp.int32)
    hcol = jnp.where((lag >= 0)[:, :, None], h_short[lag_index], 0.0)
    a8 = jnp.exp(-lam * CHUNK)
    return lam, g_tab, w_tab, hcol, a8


def local_conv(drive, hcol, w_tab, g_tab, a8):
    rows, channels = drive.shape
    modes = a8.shape[0]
    return pl.pallas_call(
        local_kernel,
        out_shape=(
            jax.ShapeDtypeStruct((rows, channels), jnp.float32),
            jax.ShapeDtypeStruct((modes, channels), jnp.float32),
        ),
        in_specs=[vmem_spec() for _ in range(5)],
        out_specs=(vmem_spec(), vmem_spec()),
        scratch_shapes=[pltpu.VMEM((modes, channels), jnp.float32)],
    )(drive, hcol, w_tab, g_tab, a8)


def gate(conv_local, query, g_tab, a8, state_in):
    rows, channels = conv_local.shape
    modes = a8.shape[0]
    return pl.pallas_call(
        gate_kernel,
        out_shape=jax.ShapeDtypeStruct((rows, channels), jnp.float32),
        in_specs=[vmem_spec() for _ in range(5)],
        out_specs=vmem_spec(),
        scratch_shapes=[pltpu.VMEM((modes, channels), jnp.float32)],
    )(conv_local, query, g_tab, a8, state_in)


def per_device(tokens, in_weight, short_filter, mode_weight, decay_rate, out_weight):
    tok_rows = tokens.shape[0]
    rim_rows = TAPS - 1
    lam, g_tab, w_tab, hcol, a8 = chunk_tables(decay_rate, mode_weight)
    taps = short_filter.astype(jnp.float32)
    full = lax.all_gather(tokens, "tensor", axis=1, tiled=True)
    projs = [
        jnp.dot(full, in_weight[:, k, :], preferred_element_type=jnp.float32).astype(jnp.bfloat16)
        for k in range(3)
    ]
    tails = jnp.stack([p[tok_rows - rim_rows :] for p in projs], 0)
    rims = shifted(tails, "context", 1)
    streams = []
    for k in range(3):
        padded = jnp.concatenate([rims[k], projs[k]], 0)
        acc = jnp.zeros(projs[k].shape, jnp.float32)
        for tap_number in range(TAPS):
            begin = rim_rows - tap_number
            acc = acc + taps[tap_number, k][None] * padded[begin : begin + tok_rows].astype(
                jnp.float32
            )
        streams.append(acc)
    query = streams[0]
    drive = streams[1] * streams[2]
    conv_local, block_end = local_conv(drive, hcol, w_tab, g_tab, a8)

    ends = lax.all_gather(block_end, "context", axis=0, tiled=False)
    me = lax.axis_index("context")
    gap = (me - 1 - jnp.arange(ends.shape[0])).astype(jnp.float32)
    factor = jnp.where(
        (gap >= 0.0)[:, None, None],
        jnp.exp(-lam[None] * (tok_rows * jnp.maximum(gap, 0.0))[:, None, None]),
        0.0,
    )
    state_in = jnp.sum(factor * ends, axis=0)

    gated = gate(conv_local, query, g_tab, a8, state_in).astype(jnp.bfloat16)
    partial_sums = jnp.dot(gated, out_weight, preferred_element_type=jnp.float32)
    return lax.psum_scatter(
        partial_sums.astype(jnp.bfloat16), "tensor", scatter_dimension=1, tiled=True
    )


def solution(mesh):
    placed = (
        P(("groups", "context"), "tensor"),
        P(None, None, "tensor"),
        P(None, None, "tensor"),
        P("tensor", None),
        P("tensor", None),
        P("tensor", None),
    )
    return jax.shard_map(
        per_device,
        mesh=mesh,
        in_specs=placed,
        out_specs=P(("groups", "context"), "tensor"),
        check_vma=False,
    )
```

```python
import jax
import jax.numpy as jnp
from jax import lax
from jax.experimental import pallas as pl
from jax.experimental.pallas import tpu as pltpu
from jax.sharding import PartitionSpec as P

TAPS = 7
CHUNK = 8


def shifted(array, axis, by):
    size = lax.axis_size(axis)
    pairs = [(i, i + by) for i in range(size) if 0 <= i + by < size]
    return lax.ppermute(array, axis, pairs)


def local_kernel(d_ref, hcol_ref, w_ref, a8_ref, conv_ref, sums_ref, end_ref, s_ref):
    rows = d_ref.shape[0]
    modes = a8_ref.shape[0]
    s_ref[...] = jnp.zeros(s_ref.shape, jnp.float32)

    def body(b, carry):
        start = pl.multiple_of(b * CHUNK, CHUNK)
        chunk = d_ref[pl.ds(start, CHUNK), :]
        acc = jnp.zeros(chunk.shape, jnp.float32)
        piece = jnp.zeros(s_ref.shape, jnp.float32)
        for j in range(CHUNK):
            row = chunk[j : j + 1, :]
            acc = acc + hcol_ref[j] * row
            piece = piece + w_ref[j] * row
        conv_ref[pl.ds(start, CHUNK), :] = acc
        sums_ref[pl.ds(pl.multiple_of(b * modes, modes), modes), :] = piece
        s_ref[...] = a8_ref[...] * s_ref[...] + piece
        return carry

    lax.fori_loop(0, rows // CHUNK, body, 0)
    end_ref[...] = s_ref[...]


def gate_kernel(conv_ref, q_ref, sums_ref, g_ref, a8_ref, sin_ref, out_ref, s_ref):
    rows = conv_ref.shape[0]
    modes = a8_ref.shape[0]
    s_ref[...] = sin_ref[...]

    def body(b, carry):
        start = pl.multiple_of(b * CHUNK, CHUNK)
        state = s_ref[...]
        acc = conv_ref[pl.ds(start, CHUNK), :]
        for n in range(modes):
            acc = acc + g_ref[n] * state[n : n + 1, :]
        out_ref[pl.ds(start, CHUNK), :] = q_ref[pl.ds(start, CHUNK), :] * acc
        piece = sums_ref[pl.ds(pl.multiple_of(b * modes, modes), modes), :]
        s_ref[...] = a8_ref[...] * state + piece
        return carry

    lax.fori_loop(0, rows // CHUNK, body, 0)


def vmem_spec():
    return pl.BlockSpec(memory_space=pltpu.VMEM)


def per_device(tokens, in_weight, short_filter, mode_weight, decay_rate, out_weight):
    tok_rows = tokens.shape[0]
    channels = in_weight.shape[2]
    modes = decay_rate.shape[1]
    proj = jnp.einsum(
        "td,dkc->tkc",
        lax.all_gather(tokens, "tensor", axis=1, tiled=True),
        in_weight,
        preferred_element_type=jnp.float32,
    ).astype(jnp.bfloat16)
    rim = shifted(proj[tok_rows - (TAPS - 1) :], "context", 1)
    padded = jnp.concatenate([rim, proj], 0)
    filtered = jnp.zeros((tok_rows, 3, channels), jnp.float32)
    for tap_number in range(TAPS):
        begin = TAPS - 1 - tap_number
        filtered = filtered + short_filter[tap_number].astype(jnp.float32)[None] * padded[
            begin : begin + tok_rows
        ].astype(jnp.float32)
    query = filtered[:, 0]
    drive = filtered[:, 1] * filtered[:, 2]

    lam = decay_rate.T
    amp = (mode_weight * jnp.sqrt(2.0 * decay_rate)).T
    steps = jnp.arange(CHUNK).astype(jnp.float32)
    g_tab = amp[:, None, :] * jnp.exp(-lam[:, None, :] * steps[None, :, None])
    w_tab = jnp.exp(-lam[None, :, :] * (CHUNK - steps)[:, None, None])
    h_short = jnp.sum(g_tab, axis=0)
    lag = steps[None, :] - steps[:, None]
    lag_index = jnp.clip(lag, 0, CHUNK - 1).astype(jnp.int32)
    hcol = jnp.where((lag >= 0)[:, :, None], h_short[lag_index], 0.0)
    a8 = jnp.exp(-lam * CHUNK)

    conv_local, sums, end_state = pl.pallas_call(
        local_kernel,
        out_shape=(
            jax.ShapeDtypeStruct((tok_rows, channels), jnp.float32),
            jax.ShapeDtypeStruct((tok_rows // CHUNK * modes, channels), jnp.float32),
            jax.ShapeDtypeStruct((modes, channels), jnp.float32),
        ),
        in_specs=[vmem_spec() for _ in range(4)],
        out_specs=(vmem_spec(), vmem_spec(), vmem_spec()),
        scratch_shapes=[pltpu.VMEM((modes, channels), jnp.float32)],
    )(drive, hcol, w_tab, a8)

    ends = lax.all_gather(end_state, "context", axis=0, tiled=False)
    block_count = ends.shape[0]
    me = lax.axis_index("context")
    gap = (me - 1 - jnp.arange(block_count)).astype(jnp.float32)
    factor = jnp.where(
        (gap >= 0.0)[:, None, None],
        jnp.exp(-lam[None] * (tok_rows * jnp.maximum(gap, 0.0))[:, None, None]),
        0.0,
    )
    state_in = jnp.sum(factor * ends, axis=0)

    gated = pl.pallas_call(
        gate_kernel,
        out_shape=jax.ShapeDtypeStruct((tok_rows, channels), jnp.float32),
        in_specs=[vmem_spec() for _ in range(6)],
        out_specs=vmem_spec(),
        scratch_shapes=[pltpu.VMEM((modes, channels), jnp.float32)],
    )(conv_local, query, sums, g_tab, a8, state_in)
    gated = gated.astype(jnp.bfloat16)
    partial_sums = jnp.dot(gated, out_weight, preferred_element_type=jnp.float32)
    summed = lax.psum_scatter(
        partial_sums.astype(jnp.bfloat16), "tensor", scatter_dimension=1, tiled=True
    )
    return summed


def solution(mesh):
    placed = (
        P(("groups", "context"), "tensor"),
        P(None, None, "tensor"),
        P(None, None, "tensor"),
        P("tensor", None),
        P("tensor", None),
        P("tensor", None),
    )
    return jax.shard_map(
        per_device,
        mesh=mesh,
        in_specs=placed,
        out_specs=P(("groups", "context"), "tensor"),
        check_vma=False,
    )
```

```python
import jax
import jax.numpy as jnp
from jax import lax
from jax.experimental import pallas as pl
from jax.experimental.pallas import tpu as pltpu
from jax.sharding import PartitionSpec as P

TAPS = 7
CHUNK = 8


def shifted(array, axis, by):
    size = lax.axis_size(axis)
    pairs = [(i, i + by) for i in range(size) if 0 <= i + by < size]
    return lax.ppermute(array, axis, pairs)


def local_kernel(d_ref, hcol_ref, w_ref, a8_ref, conv_ref, sums_ref, end_ref, s_ref):
    rows = d_ref.shape[0]
    modes = a8_ref.shape[0]
    s_ref[...] = jnp.zeros(s_ref.shape, jnp.float32)

    def body(b, carry):
        start = pl.multiple_of(b * CHUNK, CHUNK)
        chunk = d_ref[pl.ds(start, CHUNK), :]
        acc = jnp.zeros(chunk.shape, jnp.float32)
        piece = jnp.zeros(s_ref.shape, jnp.float32)
        for j in range(CHUNK):
            row = chunk[j : j + 1, :]
            acc = acc + hcol_ref[j] * row
            piece = piece + w_ref[j] * row
        conv_ref[pl.ds(start, CHUNK), :] = acc
        sums_ref[pl.ds(pl.multiple_of(b * modes, modes), modes), :] = piece
        s_ref[...] = a8_ref[...] * s_ref[...] + piece
        return carry

    lax.fori_loop(0, rows // CHUNK, body, 0)
    end_ref[...] = s_ref[...]


def gate_kernel(conv_ref, sums_ref, g_ref, a8_ref, sin_ref, out_ref, s_ref):
    rows = conv_ref.shape[0]
    modes = a8_ref.shape[0]
    s_ref[...] = sin_ref[...]

    def body(b, carry):
        start = pl.multiple_of(b * CHUNK, CHUNK)
        state = s_ref[...]
        acc = conv_ref[pl.ds(start, CHUNK), :]
        for n in range(modes):
            acc = acc + g_ref[n] * state[n : n + 1, :]
        out_ref[pl.ds(start, CHUNK), :] = acc
        piece = sums_ref[pl.ds(pl.multiple_of(b * modes, modes), modes), :]
        s_ref[...] = a8_ref[...] * state + piece
        return carry

    lax.fori_loop(0, rows // CHUNK, body, 0)


def vmem_spec():
    return pl.BlockSpec(memory_space=pltpu.VMEM)


def per_device(tokens, in_weight, short_filter, mode_weight, decay_rate, out_weight):
    tok_rows = tokens.shape[0]
    channels = in_weight.shape[2]
    modes = decay_rate.shape[1]
    proj = jnp.einsum(
        "td,dkc->tkc",
        lax.all_gather(tokens, "tensor", axis=1, tiled=True),
        in_weight,
        preferred_element_type=jnp.float32,
    ).astype(jnp.bfloat16)
    rim = shifted(proj[tok_rows - (TAPS - 1) :], "context", 1)
    padded = jnp.concatenate([rim, proj], 0)
    filtered = jnp.zeros((tok_rows, 3, channels), jnp.float32)
    for tap_number in range(TAPS):
        begin = TAPS - 1 - tap_number
        filtered = filtered + short_filter[tap_number].astype(jnp.float32)[None] * padded[
            begin : begin + tok_rows
        ].astype(jnp.float32)
    query = filtered[:, 0]
    drive = filtered[:, 1] * filtered[:, 2]

    lam = decay_rate.T
    amp = (mode_weight * jnp.sqrt(2.0 * decay_rate)).T
    steps = jnp.arange(CHUNK).astype(jnp.float32)
    g_tab = amp[:, None, :] * jnp.exp(-lam[:, None, :] * steps[None, :, None])
    w_tab = jnp.exp(-lam[None, :, :] * (CHUNK - steps)[:, None, None])
    h_short = jnp.sum(g_tab, axis=0)
    lag = steps[None, :] - steps[:, None]
    lag_index = jnp.clip(lag, 0, CHUNK - 1).astype(jnp.int32)
    hcol = jnp.where((lag >= 0)[:, :, None], h_short[lag_index], 0.0)
    a8 = jnp.exp(-lam * CHUNK)

    conv_local, sums, end_state = pl.pallas_call(
        local_kernel,
        out_shape=(
            jax.ShapeDtypeStruct((tok_rows, channels), jnp.float32),
            jax.ShapeDtypeStruct((tok_rows // CHUNK * modes, channels), jnp.float32),
            jax.ShapeDtypeStruct((modes, channels), jnp.float32),
        ),
        in_specs=[vmem_spec() for _ in range(4)],
        out_specs=(vmem_spec(), vmem_spec(), vmem_spec()),
        scratch_shapes=[pltpu.VMEM((modes, channels), jnp.float32)],
    )(drive, hcol, w_tab, a8)

    ends = lax.all_gather(end_state, "context", axis=0, tiled=False)
    block_count = ends.shape[0]
    me = lax.axis_index("context")
    gap = (me - 1 - jnp.arange(block_count)).astype(jnp.float32)
    factor = jnp.where(
        (gap >= 0.0)[:, None, None],
        jnp.exp(-lam[None] * (tok_rows * jnp.maximum(gap, 0.0))[:, None, None]),
        0.0,
    )
    state_in = jnp.sum(factor * ends, axis=0)

    gated = pl.pallas_call(
        gate_kernel,
        out_shape=jax.ShapeDtypeStruct((tok_rows, channels), jnp.float32),
        in_specs=[vmem_spec() for _ in range(5)],
        out_specs=vmem_spec(),
        scratch_shapes=[pltpu.VMEM((modes, channels), jnp.float32)],
    )(conv_local, sums, g_tab, a8, state_in)
    gated = (query * gated).astype(jnp.bfloat16)
    partial_sums = jnp.dot(gated, out_weight, preferred_element_type=jnp.float32)
    summed = lax.psum_scatter(
        partial_sums.astype(jnp.bfloat16), "tensor", scatter_dimension=1, tiled=True
    )
    return summed


def solution(mesh):
    placed = (
        P(("groups", "context"), "tensor"),
        P(None, None, "tensor"),
        P(None, None, "tensor"),
        P("tensor", None),
        P("tensor", None),
        P("tensor", None),
    )
    return jax.shard_map(
        per_device,
        mesh=mesh,
        in_specs=placed,
        out_specs=P(("groups", "context"), "tensor"),
        check_vma=False,
    )
```

```python
import jax
import jax.numpy as jnp
from jax import lax
from jax.experimental import pallas as pl
from jax.experimental.pallas import tpu as pltpu
from jax.sharding import PartitionSpec as P

TAPS = 7
CHUNK = 8


def shifted(array, axis, by):
    size = lax.axis_size(axis)
    pairs = [(i, i + by) for i in range(size) if 0 <= i + by < size]
    return lax.ppermute(array, axis, pairs)


def local_kernel(d_ref, hcol_ref, w_ref, a8_ref, conv_ref, sums_ref, end_ref, s_ref):
    rows = d_ref.shape[0]
    modes = a8_ref.shape[0]
    s_ref[...] = jnp.zeros(s_ref.shape, jnp.float32)

    def body(b, carry):
        start = pl.multiple_of(b * (2 * CHUNK), 2 * CHUNK)
        pair = d_ref[pl.ds(start, 2 * CHUNK), :]
        halves = (pair[:CHUNK], pair[CHUNK:])
        accs = [jnp.zeros(halves[0].shape, jnp.float32) for _ in range(2)]
        pieces = [jnp.zeros(s_ref.shape, jnp.float32) for _ in range(2)]
        for j in range(CHUNK):
            hj = hcol_ref[j]
            wj = w_ref[j]
            for h in range(2):
                row = halves[h][j : j + 1, :]
                accs[h] = accs[h] + hj * row
                pieces[h] = pieces[h] + wj * row
        conv_ref[pl.ds(start, 2 * CHUNK), :] = jnp.concatenate(accs, 0)
        sums_ref[pl.ds(pl.multiple_of(b * (2 * modes), 2 * modes), 2 * modes), :] = jnp.concatenate(
            pieces, 0
        )
        a8 = a8_ref[...]
        s_ref[...] = a8 * (a8 * s_ref[...] + pieces[0]) + pieces[1]
        return carry

    lax.fori_loop(0, rows // (2 * CHUNK), body, 0)
    end_ref[...] = s_ref[...]


def gate_kernel(conv_ref, q_ref, sums_ref, g_ref, a8_ref, sin_ref, out_ref, s_ref):
    rows = conv_ref.shape[0]
    modes = a8_ref.shape[0]
    s_ref[...] = sin_ref[...]

    def body(b, carry):
        start = pl.multiple_of(b * (2 * CHUNK), 2 * CHUNK)
        a8 = a8_ref[...]
        first = s_ref[...]
        pieces = sums_ref[pl.ds(pl.multiple_of(b * (2 * modes), 2 * modes), 2 * modes), :]
        second = a8 * first + pieces[:modes]
        pair = conv_ref[pl.ds(start, 2 * CHUNK), :]
        accs = [pair[:CHUNK], pair[CHUNK:]]
        for n in range(modes):
            gn = g_ref[n]
            accs[0] = accs[0] + gn * first[n : n + 1, :]
            accs[1] = accs[1] + gn * second[n : n + 1, :]
        out_ref[pl.ds(start, 2 * CHUNK), :] = q_ref[pl.ds(start, 2 * CHUNK), :] * jnp.concatenate(
            accs, 0
        )
        s_ref[...] = a8 * second + pieces[modes:]
        return carry

    lax.fori_loop(0, rows // (2 * CHUNK), body, 0)


def vmem_spec():
    return pl.BlockSpec(memory_space=pltpu.VMEM)


def per_device(tokens, in_weight, short_filter, mode_weight, decay_rate, out_weight):
    tok_rows = tokens.shape[0]
    channels = in_weight.shape[2]
    modes = decay_rate.shape[1]
    proj = jnp.einsum(
        "td,dkc->tkc",
        lax.all_gather(tokens, "tensor", axis=1, tiled=True),
        in_weight,
        preferred_element_type=jnp.float32,
    ).astype(jnp.bfloat16)
    rim = shifted(proj[tok_rows - (TAPS - 1) :], "context", 1)
    padded = jnp.concatenate([rim, proj], 0)
    filtered = jnp.zeros((tok_rows, 3, channels), jnp.float32)
    for tap_number in range(TAPS):
        begin = TAPS - 1 - tap_number
        filtered = filtered + short_filter[tap_number].astype(jnp.float32)[None] * padded[
            begin : begin + tok_rows
        ].astype(jnp.float32)
    query = filtered[:, 0]
    drive = filtered[:, 1] * filtered[:, 2]

    lam = decay_rate.T
    amp = (mode_weight * jnp.sqrt(2.0 * decay_rate)).T
    steps = jnp.arange(CHUNK).astype(jnp.float32)
    g_tab = amp[:, None, :] * jnp.exp(-lam[:, None, :] * steps[None, :, None])
    w_tab = jnp.exp(-lam[None, :, :] * (CHUNK - steps)[:, None, None])
    h_short = jnp.sum(g_tab, axis=0)
    lag = steps[None, :] - steps[:, None]
    lag_index = jnp.clip(lag, 0, CHUNK - 1).astype(jnp.int32)
    hcol = jnp.where((lag >= 0)[:, :, None], h_short[lag_index], 0.0)
    a8 = jnp.exp(-lam * CHUNK)

    conv_local, sums, end_state = pl.pallas_call(
        local_kernel,
        out_shape=(
            jax.ShapeDtypeStruct((tok_rows, channels), jnp.float32),
            jax.ShapeDtypeStruct((tok_rows // CHUNK * modes, channels), jnp.float32),
            jax.ShapeDtypeStruct((modes, channels), jnp.float32),
        ),
        in_specs=[vmem_spec() for _ in range(4)],
        out_specs=(vmem_spec(), vmem_spec(), vmem_spec()),
        scratch_shapes=[pltpu.VMEM((modes, channels), jnp.float32)],
    )(drive, hcol, w_tab, a8)

    ends = lax.all_gather(end_state, "context", axis=0, tiled=False)
    block_count = ends.shape[0]
    me = lax.axis_index("context")
    gap = (me - 1 - jnp.arange(block_count)).astype(jnp.float32)
    factor = jnp.where(
        (gap >= 0.0)[:, None, None],
        jnp.exp(-lam[None] * (tok_rows * jnp.maximum(gap, 0.0))[:, None, None]),
        0.0,
    )
    state_in = jnp.sum(factor * ends, axis=0)

    gated = pl.pallas_call(
        gate_kernel,
        out_shape=jax.ShapeDtypeStruct((tok_rows, channels), jnp.float32),
        in_specs=[vmem_spec() for _ in range(6)],
        out_specs=vmem_spec(),
        scratch_shapes=[pltpu.VMEM((modes, channels), jnp.float32)],
    )(conv_local, query, sums, g_tab, a8, state_in)
    gated = gated.astype(jnp.bfloat16)
    partial_sums = jnp.dot(gated, out_weight, preferred_element_type=jnp.float32)
    summed = lax.psum_scatter(
        partial_sums.astype(jnp.bfloat16), "tensor", scatter_dimension=1, tiled=True
    )
    return summed


def solution(mesh):
    placed = (
        P(("groups", "context"), "tensor"),
        P(None, None, "tensor"),
        P(None, None, "tensor"),
        P("tensor", None),
        P("tensor", None),
        P("tensor", None),
    )
    return jax.shard_map(
        per_device,
        mesh=mesh,
        in_specs=placed,
        out_specs=P(("groups", "context"), "tensor"),
        check_vma=False,
    )
```

```python
import jax
import jax.numpy as jnp
from jax import lax
from jax.experimental import pallas as pl
from jax.experimental.pallas import tpu as pltpu
from jax.sharding import PartitionSpec as P

TAPS = 7
CHUNK = 8


def shifted(array, axis, by):
    size = lax.axis_size(axis)
    pairs = [(i, i + by) for i in range(size) if 0 <= i + by < size]
    return lax.ppermute(array, axis, pairs)


def local_kernel(d_ref, hcol_ref, w_ref, a8_ref, conv_ref, sums_ref, end_ref, s_ref):
    rows = d_ref.shape[0]
    modes = a8_ref.shape[0]
    s_ref[...] = jnp.zeros(s_ref.shape, jnp.float32)

    def body(b, carry):
        start = pl.multiple_of(b * CHUNK, CHUNK)
        chunk = d_ref[pl.ds(start, CHUNK), :]
        acc = jnp.zeros(chunk.shape, jnp.float32)
        piece = jnp.zeros(s_ref.shape, jnp.float32)
        for j in range(CHUNK):
            row = chunk[j : j + 1, :]
            acc = acc + hcol_ref[j] * row
            piece = piece + w_ref[j] * row
        conv_ref[pl.ds(start, CHUNK), :] = acc
        sums_ref[pl.ds(pl.multiple_of(b * modes, modes), modes), :] = piece
        s_ref[...] = a8_ref[...] * s_ref[...] + piece
        return carry

    lax.fori_loop(0, rows // CHUNK, body, 0, unroll=4)
    end_ref[...] = s_ref[...]


def gate_kernel(conv_ref, q_ref, sums_ref, g_ref, a8_ref, sin_ref, out_ref, s_ref):
    rows = conv_ref.shape[0]
    modes = a8_ref.shape[0]
    s_ref[...] = sin_ref[...]

    def body(b, carry):
        start = pl.multiple_of(b * CHUNK, CHUNK)
        state = s_ref[...]
        acc = conv_ref[pl.ds(start, CHUNK), :]
        for n in range(modes):
            acc = acc + g_ref[n] * state[n : n + 1, :]
        out_ref[pl.ds(start, CHUNK), :] = q_ref[pl.ds(start, CHUNK), :] * acc
        piece = sums_ref[pl.ds(pl.multiple_of(b * modes, modes), modes), :]
        s_ref[...] = a8_ref[...] * state + piece
        return carry

    lax.fori_loop(0, rows // CHUNK, body, 0, unroll=4)


def vmem_spec():
    return pl.BlockSpec(memory_space=pltpu.VMEM)


def per_device(tokens, in_weight, short_filter, mode_weight, decay_rate, out_weight):
    tok_rows = tokens.shape[0]
    channels = in_weight.shape[2]
    modes = decay_rate.shape[1]
    proj = jnp.einsum(
        "td,dkc->tkc",
        lax.all_gather(tokens, "tensor", axis=1, tiled=True),
        in_weight,
        preferred_element_type=jnp.float32,
    ).astype(jnp.bfloat16)
    rim = shifted(proj[tok_rows - (TAPS - 1) :], "context", 1)
    padded = jnp.concatenate([rim, proj], 0)
    filtered = jnp.zeros((tok_rows, 3, channels), jnp.float32)
    for tap_number in range(TAPS):
        begin = TAPS - 1 - tap_number
        filtered = filtered + short_filter[tap_number].astype(jnp.float32)[None] * padded[
            begin : begin + tok_rows
        ].astype(jnp.float32)
    query = filtered[:, 0]
    drive = filtered[:, 1] * filtered[:, 2]

    lam = decay_rate.T
    amp = (mode_weight * jnp.sqrt(2.0 * decay_rate)).T
    steps = jnp.arange(CHUNK).astype(jnp.float32)
    g_tab = amp[:, None, :] * jnp.exp(-lam[:, None, :] * steps[None, :, None])
    w_tab = jnp.exp(-lam[None, :, :] * (CHUNK - steps)[:, None, None])
    h_short = jnp.sum(g_tab, axis=0)
    lag = steps[None, :] - steps[:, None]
    lag_index = jnp.clip(lag, 0, CHUNK - 1).astype(jnp.int32)
    hcol = jnp.where((lag >= 0)[:, :, None], h_short[lag_index], 0.0)
    a8 = jnp.exp(-lam * CHUNK)

    conv_local, sums, end_state = pl.pallas_call(
        local_kernel,
        out_shape=(
            jax.ShapeDtypeStruct((tok_rows, channels), jnp.float32),
            jax.ShapeDtypeStruct((tok_rows // CHUNK * modes, channels), jnp.float32),
            jax.ShapeDtypeStruct((modes, channels), jnp.float32),
        ),
        in_specs=[vmem_spec() for _ in range(4)],
        out_specs=(vmem_spec(), vmem_spec(), vmem_spec()),
        scratch_shapes=[pltpu.VMEM((modes, channels), jnp.float32)],
    )(drive, hcol, w_tab, a8)

    ends = lax.all_gather(end_state, "context", axis=0, tiled=False)
    block_count = ends.shape[0]
    me = lax.axis_index("context")
    gap = (me - 1 - jnp.arange(block_count)).astype(jnp.float32)
    factor = jnp.where(
        (gap >= 0.0)[:, None, None],
        jnp.exp(-lam[None] * (tok_rows * jnp.maximum(gap, 0.0))[:, None, None]),
        0.0,
    )
    state_in = jnp.sum(factor * ends, axis=0)

    gated = pl.pallas_call(
        gate_kernel,
        out_shape=jax.ShapeDtypeStruct((tok_rows, channels), jnp.float32),
        in_specs=[vmem_spec() for _ in range(6)],
        out_specs=vmem_spec(),
        scratch_shapes=[pltpu.VMEM((modes, channels), jnp.float32)],
    )(conv_local, query, sums, g_tab, a8, state_in)
    gated = gated.astype(jnp.bfloat16)
    partial_sums = jnp.dot(gated, out_weight, preferred_element_type=jnp.float32)
    summed = lax.psum_scatter(
        partial_sums.astype(jnp.bfloat16), "tensor", scatter_dimension=1, tiled=True
    )
    return summed


def solution(mesh):
    placed = (
        P(("groups", "context"), "tensor"),
        P(None, None, "tensor"),
        P(None, None, "tensor"),
        P("tensor", None),
        P("tensor", None),
        P("tensor", None),
    )
    return jax.shard_map(
        per_device,
        mesh=mesh,
        in_specs=placed,
        out_specs=P(("groups", "context"), "tensor"),
        check_vma=False,
    )
```

```python
import jax
import jax.numpy as jnp
from jax import lax
from jax.experimental import pallas as pl
from jax.experimental.pallas import tpu as pltpu
from jax.sharding import PartitionSpec as P

TAPS = 7
CHUNK = 8


def shifted(array, axis, by):
    size = lax.axis_size(axis)
    pairs = [(i, i + by) for i in range(size) if 0 <= i + by < size]
    return lax.ppermute(array, axis, pairs)


BLOCK = 128


def local_kernel(d_ref, hcol_ref, w_ref, a8_ref, conv_ref, sums_ref, end_ref, s_ref):
    rows = d_ref.shape[0]
    modes = a8_ref.shape[0]

    @pl.when(pl.program_id(0) == 0)
    def _():
        s_ref[...] = jnp.zeros(s_ref.shape, jnp.float32)

    def body(b, carry):
        start = pl.multiple_of(b * CHUNK, CHUNK)
        chunk = d_ref[pl.ds(start, CHUNK), :]
        acc = jnp.zeros(chunk.shape, jnp.float32)
        piece = jnp.zeros(s_ref.shape, jnp.float32)
        for j in range(CHUNK):
            row = chunk[j : j + 1, :]
            acc = acc + hcol_ref[j] * row
            piece = piece + w_ref[j] * row
        conv_ref[pl.ds(start, CHUNK), :] = acc
        sums_ref[pl.ds(pl.multiple_of(b * modes, modes), modes), :] = piece
        s_ref[...] = a8_ref[...] * s_ref[...] + piece
        return carry

    lax.fori_loop(0, rows // CHUNK, body, 0, unroll=4)
    end_ref[...] = s_ref[...]


def gate_kernel(conv_ref, q_ref, sums_ref, g_ref, a8_ref, sin_ref, out_ref, s_ref):
    rows = conv_ref.shape[0]
    modes = a8_ref.shape[0]

    @pl.when(pl.program_id(0) == 0)
    def _():
        s_ref[...] = sin_ref[...]

    def body(b, carry):
        start = pl.multiple_of(b * CHUNK, CHUNK)
        state = s_ref[...]
        acc = conv_ref[pl.ds(start, CHUNK), :]
        for n in range(modes):
            acc = acc + g_ref[n] * state[n : n + 1, :]
        out_ref[pl.ds(start, CHUNK), :] = q_ref[pl.ds(start, CHUNK), :] * acc
        piece = sums_ref[pl.ds(pl.multiple_of(b * modes, modes), modes), :]
        s_ref[...] = a8_ref[...] * state + piece
        return carry

    lax.fori_loop(0, rows // CHUNK, body, 0, unroll=4)


def rows_spec(rows, channels):
    return pl.BlockSpec((rows, channels), lambda i: (i, 0))


def whole_spec(shape):
    return pl.BlockSpec(shape, lambda i: (0,) * len(shape))


def sequential():
    return pltpu.CompilerParams(dimension_semantics=("arbitrary",))


def chunk_tables(decay_rate, mode_weight):
    lam = decay_rate.T
    amp = (mode_weight * jnp.sqrt(2.0 * decay_rate)).T
    steps = jnp.arange(CHUNK).astype(jnp.float32)
    g_tab = amp[:, None, :] * jnp.exp(-lam[:, None, :] * steps[None, :, None])
    w_tab = jnp.exp(-lam[None, :, :] * (CHUNK - steps)[:, None, None])
    h_short = jnp.sum(g_tab, axis=0)
    lag = steps[None, :] - steps[:, None]
    lag_index = jnp.clip(lag, 0, CHUNK - 1).astype(jnp.int32)
    hcol = jnp.where((lag >= 0)[:, :, None], h_short[lag_index], 0.0)
    a8 = jnp.exp(-lam * CHUNK)
    return lam, g_tab, w_tab, hcol, a8


def local_conv(drive, hcol, w_tab, a8):
    rows, channels = drive.shape
    modes = a8.shape[0]
    blk = min(BLOCK, rows)
    per = blk // CHUNK * modes
    return pl.pallas_call(
        local_kernel,
        grid=(rows // blk,),
        out_shape=(
            jax.ShapeDtypeStruct((rows, channels), jnp.float32),
            jax.ShapeDtypeStruct((rows // CHUNK * modes, channels), jnp.float32),
            jax.ShapeDtypeStruct((modes, channels), jnp.float32),
        ),
        in_specs=[
            rows_spec(blk, channels),
            whole_spec(hcol.shape),
            whole_spec(w_tab.shape),
            whole_spec(a8.shape),
        ],
        out_specs=(rows_spec(blk, channels), rows_spec(per, channels), whole_spec(a8.shape)),
        scratch_shapes=[pltpu.VMEM((modes, channels), jnp.float32)],
        compiler_params=sequential(),
    )(drive, hcol, w_tab, a8)


def gate(conv_local, query, sums, g_tab, a8, state_in):
    rows, channels = conv_local.shape
    modes = a8.shape[0]
    blk = min(BLOCK, rows)
    per = blk // CHUNK * modes
    return pl.pallas_call(
        gate_kernel,
        grid=(rows // blk,),
        out_shape=jax.ShapeDtypeStruct((rows, channels), jnp.float32),
        in_specs=[
            rows_spec(blk, channels),
            rows_spec(blk, channels),
            rows_spec(per, channels),
            whole_spec(g_tab.shape),
            whole_spec(a8.shape),
            whole_spec(state_in.shape),
        ],
        out_specs=rows_spec(blk, channels),
        scratch_shapes=[pltpu.VMEM((modes, channels), jnp.float32)],
        compiler_params=sequential(),
    )(conv_local, query, sums, g_tab, a8, state_in)


def per_device(tokens, in_weight, short_filter, mode_weight, decay_rate, out_weight):
    tok_rows = tokens.shape[0]
    channels = in_weight.shape[2]
    proj = jnp.einsum(
        "td,dkc->tkc",
        lax.all_gather(tokens, "tensor", axis=1, tiled=True),
        in_weight,
        preferred_element_type=jnp.float32,
    ).astype(jnp.bfloat16)
    rim = shifted(proj[tok_rows - (TAPS - 1) :], "context", 1)
    padded = jnp.concatenate([rim, proj], 0)
    filtered = jnp.zeros((tok_rows, 3, channels), jnp.float32)
    for tap_number in range(TAPS):
        begin = TAPS - 1 - tap_number
        filtered = filtered + short_filter[tap_number].astype(jnp.float32)[None] * padded[
            begin : begin + tok_rows
        ].astype(jnp.float32)
    query = filtered[:, 0]
    drive = filtered[:, 1] * filtered[:, 2]

    lam, g_tab, w_tab, hcol, a8 = chunk_tables(decay_rate, mode_weight)
    conv_local, sums, end_state = local_conv(drive, hcol, w_tab, a8)

    ends = lax.all_gather(end_state, "context", axis=0, tiled=False)
    block_count = ends.shape[0]
    me = lax.axis_index("context")
    gap = (me - 1 - jnp.arange(block_count)).astype(jnp.float32)
    factor = jnp.where(
        (gap >= 0.0)[:, None, None],
        jnp.exp(-lam[None] * (tok_rows * jnp.maximum(gap, 0.0))[:, None, None]),
        0.0,
    )
    state_in = jnp.sum(factor * ends, axis=0)

    gated = gate(conv_local, query, sums, g_tab, a8, state_in)
    gated = gated.astype(jnp.bfloat16)
    partial_sums = jnp.dot(gated, out_weight, preferred_element_type=jnp.float32)
    summed = lax.psum_scatter(
        partial_sums.astype(jnp.bfloat16), "tensor", scatter_dimension=1, tiled=True
    )
    return summed


def solution(mesh):
    placed = (
        P(("groups", "context"), "tensor"),
        P(None, None, "tensor"),
        P(None, None, "tensor"),
        P("tensor", None),
        P("tensor", None),
        P("tensor", None),
    )
    return jax.shard_map(
        per_device,
        mesh=mesh,
        in_specs=placed,
        out_specs=P(("groups", "context"), "tensor"),
        check_vma=False,
    )
```

```python
import jax
import jax.numpy as jnp
from jax import lax
from jax.experimental import pallas as pl
from jax.experimental.pallas import tpu as pltpu
from jax.sharding import PartitionSpec as P

TAPS = 7
CHUNK = 8


def shifted(array, axis, by):
    size = lax.axis_size(axis)
    pairs = [(i, i + by) for i in range(size) if 0 <= i + by < size]
    return lax.ppermute(array, axis, pairs)


BLOCK = 128


def local_kernel(d_ref, hcol_ref, w_ref, a8_ref, conv_ref, sums_ref, end_ref, s_ref):
    rows = d_ref.shape[0]
    modes = a8_ref.shape[0]

    @pl.when(pl.program_id(0) == 0)
    def _():
        s_ref[...] = jnp.zeros(s_ref.shape, jnp.float32)

    def body(b, carry):
        start = pl.multiple_of(b * CHUNK, CHUNK)
        chunk = d_ref[pl.ds(start, CHUNK), :]
        acc = jnp.zeros(chunk.shape, jnp.float32)
        piece = jnp.zeros(s_ref.shape, jnp.float32)
        for j in range(CHUNK):
            row = chunk[j : j + 1, :]
            acc = acc + hcol_ref[j] * row
            piece = piece + w_ref[j] * row
        conv_ref[pl.ds(start, CHUNK), :] = acc
        sums_ref[pl.ds(pl.multiple_of(b * modes, modes), modes), :] = piece
        s_ref[...] = a8_ref[...] * s_ref[...] + piece
        return carry

    lax.fori_loop(0, rows // CHUNK, body, 0, unroll=4)
    end_ref[...] = s_ref[...]


def gate_kernel(conv_ref, q_ref, sums_ref, g_ref, a8_ref, sin_ref, out_ref, s_ref):
    rows = conv_ref.shape[0]
    modes = a8_ref.shape[0]

    @pl.when(pl.program_id(0) == 0)
    def _():
        s_ref[...] = sin_ref[...]

    def body(b, carry):
        start = pl.multiple_of(b * CHUNK, CHUNK)
        state = s_ref[...]
        acc = conv_ref[pl.ds(start, CHUNK), :]
        for n in range(modes):
            acc = acc + g_ref[n] * state[n : n + 1, :]
        out_ref[pl.ds(start, CHUNK), :] = q_ref[pl.ds(start, CHUNK), :] * acc
        piece = sums_ref[pl.ds(pl.multiple_of(b * modes, modes), modes), :]
        s_ref[...] = a8_ref[...] * state + piece
        return carry

    lax.fori_loop(0, rows // CHUNK, body, 0, unroll=4)


def rows_spec(rows, channels):
    return pl.BlockSpec((rows, channels), lambda i: (i, 0))


def whole_spec(shape):
    return pl.BlockSpec(shape, lambda i: (0,) * len(shape))


def sequential():
    return pltpu.CompilerParams(dimension_semantics=("arbitrary",))


def chunk_tables(decay_rate, mode_weight):
    lam = decay_rate.T
    amp = (mode_weight * jnp.sqrt(2.0 * decay_rate)).T
    steps = jnp.arange(CHUNK).astype(jnp.float32)
    g_tab = amp[:, None, :] * jnp.exp(-lam[:, None, :] * steps[None, :, None])
    w_tab = jnp.exp(-lam[None, :, :] * (CHUNK - steps)[:, None, None])
    h_short = jnp.sum(g_tab, axis=0)
    lag = steps[None, :] - steps[:, None]
    lag_index = jnp.clip(lag, 0, CHUNK - 1).astype(jnp.int32)
    hcol = jnp.where((lag >= 0)[:, :, None], h_short[lag_index], 0.0)
    a8 = jnp.exp(-lam * CHUNK)
    return lam, g_tab, w_tab, hcol, a8


def local_conv(drive, hcol, w_tab, a8):
    rows, channels = drive.shape
    modes = a8.shape[0]
    blk = min(BLOCK, rows)
    per = blk // CHUNK * modes
    return pl.pallas_call(
        local_kernel,
        grid=(rows // blk,),
        out_shape=(
            jax.ShapeDtypeStruct((rows, channels), jnp.float32),
            jax.ShapeDtypeStruct((rows // CHUNK * modes, channels), jnp.float32),
            jax.ShapeDtypeStruct((modes, channels), jnp.float32),
        ),
        in_specs=[
            rows_spec(blk, channels),
            whole_spec(hcol.shape),
            whole_spec(w_tab.shape),
            whole_spec(a8.shape),
        ],
        out_specs=(rows_spec(blk, channels), rows_spec(per, channels), whole_spec(a8.shape)),
        scratch_shapes=[pltpu.VMEM((modes, channels), jnp.float32)],
        compiler_params=sequential(),
    )(drive, hcol, w_tab, a8)


def gate(conv_local, query, sums, g_tab, a8, state_in):
    rows, channels = conv_local.shape
    modes = a8.shape[0]
    blk = min(BLOCK, rows)
    per = blk // CHUNK * modes
    return pl.pallas_call(
        gate_kernel,
        grid=(rows // blk,),
        out_shape=jax.ShapeDtypeStruct((rows, channels), jnp.float32),
        in_specs=[
            rows_spec(blk, channels),
            rows_spec(blk, channels),
            rows_spec(per, channels),
            whole_spec(g_tab.shape),
            whole_spec(a8.shape),
            whole_spec(state_in.shape),
        ],
        out_specs=rows_spec(blk, channels),
        scratch_shapes=[pltpu.VMEM((modes, channels), jnp.float32)],
        compiler_params=sequential(),
    )(conv_local, query, sums, g_tab, a8, state_in)


def per_device(tokens, in_weight, short_filter, mode_weight, decay_rate, out_weight):
    tok_rows = tokens.shape[0]
    channels = in_weight.shape[2]
    proj = jnp.einsum(
        "td,dkc->tkc",
        lax.all_gather(tokens, "tensor", axis=1, tiled=True),
        in_weight,
        preferred_element_type=jnp.float32,
    ).astype(jnp.bfloat16)
    rim = shifted(proj[tok_rows - (TAPS - 1) :], "context", 1)
    padded = jnp.concatenate([rim, proj], 0)
    taps = short_filter.astype(jnp.float32)

    def stream(k):
        acc = jnp.zeros((tok_rows, channels), jnp.float32)
        for tap_number in range(TAPS):
            begin = TAPS - 1 - tap_number
            acc = acc + taps[tap_number, k][None] * padded[begin : begin + tok_rows, k].astype(
                jnp.float32
            )
        return acc

    query = stream(0)
    drive = stream(1) * stream(2)

    lam, g_tab, w_tab, hcol, a8 = chunk_tables(decay_rate, mode_weight)
    conv_local, sums, end_state = local_conv(drive, hcol, w_tab, a8)

    ends = lax.all_gather(end_state, "context", axis=0, tiled=False)
    block_count = ends.shape[0]
    me = lax.axis_index("context")
    gap = (me - 1 - jnp.arange(block_count)).astype(jnp.float32)
    factor = jnp.where(
        (gap >= 0.0)[:, None, None],
        jnp.exp(-lam[None] * (tok_rows * jnp.maximum(gap, 0.0))[:, None, None]),
        0.0,
    )
    state_in = jnp.sum(factor * ends, axis=0)

    gated = gate(conv_local, query, sums, g_tab, a8, state_in)
    gated = gated.astype(jnp.bfloat16)
    partial_sums = jnp.dot(gated, out_weight, preferred_element_type=jnp.float32)
    summed = lax.psum_scatter(
        partial_sums.astype(jnp.bfloat16), "tensor", scatter_dimension=1, tiled=True
    )
    return summed


def solution(mesh):
    placed = (
        P(("groups", "context"), "tensor"),
        P(None, None, "tensor"),
        P(None, None, "tensor"),
        P("tensor", None),
        P("tensor", None),
        P("tensor", None),
    )
    return jax.shard_map(
        per_device,
        mesh=mesh,
        in_specs=placed,
        out_specs=P(("groups", "context"), "tensor"),
        check_vma=False,
    )
```

```python
import jax
import jax.numpy as jnp
from jax import lax
from jax.experimental import pallas as pl
from jax.experimental.pallas import tpu as pltpu
from jax.sharding import PartitionSpec as P

TAPS = 7
CHUNK = 8


def shifted(array, axis, by):
    size = lax.axis_size(axis)
    pairs = [(i, i + by) for i in range(size) if 0 <= i + by < size]
    return lax.ppermute(array, axis, pairs)


BLOCK = 128


def local_kernel(d_ref, hcol_ref, w_ref, a8_ref, conv_ref, sums_ref, end_ref, s_ref):
    rows = d_ref.shape[0]
    modes = a8_ref.shape[0]

    @pl.when(pl.program_id(0) == 0)
    def _():
        s_ref[...] = jnp.zeros(s_ref.shape, jnp.float32)

    def body(b, carry):
        start = pl.multiple_of(b * CHUNK, CHUNK)
        chunk = d_ref[pl.ds(start, CHUNK), :]
        acc = jnp.zeros(chunk.shape, jnp.float32)
        piece = jnp.zeros(s_ref.shape, jnp.float32)
        for j in range(CHUNK):
            row = chunk[j : j + 1, :]
            acc = acc + hcol_ref[j] * row
            piece = piece + w_ref[j] * row
        conv_ref[pl.ds(start, CHUNK), :] = acc
        sums_ref[pl.ds(pl.multiple_of(b * modes, modes), modes), :] = piece
        s_ref[...] = a8_ref[...] * s_ref[...] + piece
        return carry

    lax.fori_loop(0, rows // CHUNK, body, 0, unroll=4)
    end_ref[...] = s_ref[...]


def gate_kernel(conv_ref, q_ref, sums_ref, g_ref, a8_ref, sin_ref, wo_ref, out_ref, s_ref, gated_ref):
    rows = conv_ref.shape[0]
    modes = a8_ref.shape[0]

    @pl.when(pl.program_id(0) == 0)
    def _():
        s_ref[...] = sin_ref[...]

    def body(b, carry):
        start = pl.multiple_of(b * CHUNK, CHUNK)
        state = s_ref[...]
        acc = conv_ref[pl.ds(start, CHUNK), :]
        for n in range(modes):
            acc = acc + g_ref[n] * state[n : n + 1, :]
        gated_ref[pl.ds(start, CHUNK), :] = q_ref[pl.ds(start, CHUNK), :] * acc
        piece = sums_ref[pl.ds(pl.multiple_of(b * modes, modes), modes), :]
        s_ref[...] = a8_ref[...] * state + piece
        return carry

    lax.fori_loop(0, rows // CHUNK, body, 0, unroll=4)
    gated = gated_ref[...].astype(jnp.bfloat16)
    out_ref[...] = lax.dot_general(
        wo_ref[...], gated, (((0,), (1,)), ((), ())), preferred_element_type=jnp.float32
    ).astype(out_ref.dtype)


def rows_spec(rows, channels):
    return pl.BlockSpec((rows, channels), lambda i: (i, 0))


def whole_spec(shape):
    return pl.BlockSpec(shape, lambda i: (0,) * len(shape))


def sequential():
    return pltpu.CompilerParams(dimension_semantics=("arbitrary",))


def chunk_tables(decay_rate, mode_weight):
    lam = decay_rate.T
    amp = (mode_weight * jnp.sqrt(2.0 * decay_rate)).T
    steps = jnp.arange(CHUNK).astype(jnp.float32)
    g_tab = amp[:, None, :] * jnp.exp(-lam[:, None, :] * steps[None, :, None])
    w_tab = jnp.exp(-lam[None, :, :] * (CHUNK - steps)[:, None, None])
    h_short = jnp.sum(g_tab, axis=0)
    lag = steps[None, :] - steps[:, None]
    lag_index = jnp.clip(lag, 0, CHUNK - 1).astype(jnp.int32)
    hcol = jnp.where((lag >= 0)[:, :, None], h_short[lag_index], 0.0)
    a8 = jnp.exp(-lam * CHUNK)
    return lam, g_tab, w_tab, hcol, a8


def local_conv(drive, hcol, w_tab, a8):
    rows, channels = drive.shape
    modes = a8.shape[0]
    blk = min(BLOCK, rows)
    per = blk // CHUNK * modes
    return pl.pallas_call(
        local_kernel,
        grid=(rows // blk,),
        out_shape=(
            jax.ShapeDtypeStruct((rows, channels), jnp.float32),
            jax.ShapeDtypeStruct((rows // CHUNK * modes, channels), jnp.float32),
            jax.ShapeDtypeStruct((modes, channels), jnp.float32),
        ),
        in_specs=[
            rows_spec(blk, channels),
            whole_spec(hcol.shape),
            whole_spec(w_tab.shape),
            whole_spec(a8.shape),
        ],
        out_specs=(rows_spec(blk, channels), rows_spec(per, channels), whole_spec(a8.shape)),
        scratch_shapes=[pltpu.VMEM((modes, channels), jnp.float32)],
        compiler_params=sequential(),
    )(drive, hcol, w_tab, a8)


def gate(conv_local, query, sums, g_tab, a8, state_in, out_weight):
    rows, channels = conv_local.shape
    width = out_weight.shape[1]
    modes = a8.shape[0]
    blk = min(BLOCK, rows)
    per = blk // CHUNK * modes
    return pl.pallas_call(
        gate_kernel,
        grid=(rows // blk,),
        out_shape=jax.ShapeDtypeStruct((width, rows), jnp.bfloat16),
        in_specs=[
            rows_spec(blk, channels),
            rows_spec(blk, channels),
            rows_spec(per, channels),
            whole_spec(g_tab.shape),
            whole_spec(a8.shape),
            whole_spec(state_in.shape),
            whole_spec(out_weight.shape),
        ],
        out_specs=pl.BlockSpec((width, blk), lambda i: (0, i)),
        scratch_shapes=[
            pltpu.VMEM((modes, channels), jnp.float32),
            pltpu.VMEM((blk, channels), jnp.float32),
        ],
        compiler_params=sequential(),
    )(conv_local, query, sums, g_tab, a8, state_in, out_weight)


def per_device(tokens, in_weight, short_filter, mode_weight, decay_rate, out_weight):
    tok_rows = tokens.shape[0]
    channels = in_weight.shape[2]
    proj = jnp.einsum(
        "td,dkc->tkc",
        lax.all_gather(tokens, "tensor", axis=1, tiled=True),
        in_weight,
        preferred_element_type=jnp.float32,
    ).astype(jnp.bfloat16)
    rim = shifted(proj[tok_rows - (TAPS - 1) :], "context", 1)
    padded = jnp.concatenate([rim, proj], 0)
    filtered = jnp.zeros((tok_rows, 3, channels), jnp.float32)
    for tap_number in range(TAPS):
        begin = TAPS - 1 - tap_number
        filtered = filtered + short_filter[tap_number].astype(jnp.float32)[None] * padded[
            begin : begin + tok_rows
        ].astype(jnp.float32)
    query = filtered[:, 0]
    drive = filtered[:, 1] * filtered[:, 2]

    lam, g_tab, w_tab, hcol, a8 = chunk_tables(decay_rate, mode_weight)
    conv_local, sums, end_state = local_conv(drive, hcol, w_tab, a8)

    ends = lax.all_gather(end_state, "context", axis=0, tiled=False)
    block_count = ends.shape[0]
    me = lax.axis_index("context")
    gap = (me - 1 - jnp.arange(block_count)).astype(jnp.float32)
    factor = jnp.where(
        (gap >= 0.0)[:, None, None],
        jnp.exp(-lam[None] * (tok_rows * jnp.maximum(gap, 0.0))[:, None, None]),
        0.0,
    )
    state_in = jnp.sum(factor * ends, axis=0)

    partial_sums = gate(conv_local, query, sums, g_tab, a8, state_in, out_weight)
    summed = lax.psum_scatter(partial_sums, "tensor", scatter_dimension=0, tiled=True).T
    return summed


def solution(mesh):
    placed = (
        P(("groups", "context"), "tensor"),
        P(None, None, "tensor"),
        P(None, None, "tensor"),
        P("tensor", None),
        P("tensor", None),
        P("tensor", None),
    )
    return jax.shard_map(
        per_device,
        mesh=mesh,
        in_specs=placed,
        out_specs=P(("groups", "context"), "tensor"),
        check_vma=False,
    )
```

```python
import jax
import jax.numpy as jnp
from jax import lax
from jax.experimental import pallas as pl
from jax.experimental.pallas import tpu as pltpu
from jax.sharding import PartitionSpec as P

TAPS = 7
CHUNK = 8


def shifted(array, axis, by):
    size = lax.axis_size(axis)
    pairs = [(i, i + by) for i in range(size) if 0 <= i + by < size]
    return lax.ppermute(array, axis, pairs)


BLOCK = 256


def local_kernel(d_ref, hcol_ref, w_ref, a8_ref, conv_ref, sums_ref, end_ref, s_ref):
    rows = d_ref.shape[0]
    modes = a8_ref.shape[0]

    @pl.when(pl.program_id(0) == 0)
    def _():
        s_ref[...] = jnp.zeros(s_ref.shape, jnp.float32)

    def body(b, carry):
        start = pl.multiple_of(b * CHUNK, CHUNK)
        chunk = d_ref[pl.ds(start, CHUNK), :]
        acc = jnp.zeros(chunk.shape, jnp.float32)
        piece = jnp.zeros(s_ref.shape, jnp.float32)
        for j in range(CHUNK):
            row = chunk[j : j + 1, :]
            acc = acc + hcol_ref[j] * row
            piece = piece + w_ref[j] * row
        conv_ref[pl.ds(start, CHUNK), :] = acc
        sums_ref[pl.ds(pl.multiple_of(b * modes, modes), modes), :] = piece
        s_ref[...] = a8_ref[...] * s_ref[...] + piece
        return carry

    lax.fori_loop(0, rows // CHUNK, body, 0, unroll=4)
    end_ref[...] = s_ref[...]


def gate_kernel(conv_ref, q_ref, sums_ref, g_ref, a8_ref, sin_ref, wo_ref, out_ref, s_ref, gated_ref):
    rows = conv_ref.shape[0]
    modes = a8_ref.shape[0]

    @pl.when(pl.program_id(0) == 0)
    def _():
        s_ref[...] = sin_ref[...]

    def body(b, carry):
        start = pl.multiple_of(b * CHUNK, CHUNK)
        state = s_ref[...]
        acc = conv_ref[pl.ds(start, CHUNK), :]
        for n in range(modes):
            acc = acc + g_ref[n] * state[n : n + 1, :]
        gated_ref[pl.ds(start, CHUNK), :] = q_ref[pl.ds(start, CHUNK), :] * acc
        piece = sums_ref[pl.ds(pl.multiple_of(b * modes, modes), modes), :]
        s_ref[...] = a8_ref[...] * state + piece
        return carry

    lax.fori_loop(0, rows // CHUNK, body, 0, unroll=4)
    gated = gated_ref[...].astype(jnp.bfloat16)
    out_ref[...] = lax.dot_general(
        wo_ref[...], gated, (((0,), (1,)), ((), ())), preferred_element_type=jnp.float32
    ).astype(out_ref.dtype)


def rows_spec(rows, channels):
    return pl.BlockSpec((rows, channels), lambda i: (i, 0))


def whole_spec(shape):
    return pl.BlockSpec(shape, lambda i: (0,) * len(shape))


def sequential():
    return pltpu.CompilerParams(dimension_semantics=("arbitrary",))


def chunk_tables(decay_rate, mode_weight):
    lam = decay_rate.T
    amp = (mode_weight * jnp.sqrt(2.0 * decay_rate)).T
    steps = jnp.arange(CHUNK).astype(jnp.float32)
    g_tab = amp[:, None, :] * jnp.exp(-lam[:, None, :] * steps[None, :, None])
    w_tab = jnp.exp(-lam[None, :, :] * (CHUNK - steps)[:, None, None])
    h_short = jnp.sum(g_tab, axis=0)
    lag = steps[None, :] - steps[:, None]
    lag_index = jnp.clip(lag, 0, CHUNK - 1).astype(jnp.int32)
    hcol = jnp.where((lag >= 0)[:, :, None], h_short[lag_index], 0.0)
    a8 = jnp.exp(-lam * CHUNK)
    return lam, g_tab, w_tab, hcol, a8


def local_conv(drive, hcol, w_tab, a8):
    rows, channels = drive.shape
    modes = a8.shape[0]
    blk = min(BLOCK, rows)
    per = blk // CHUNK * modes
    return pl.pallas_call(
        local_kernel,
        grid=(rows // blk,),
        out_shape=(
            jax.ShapeDtypeStruct((rows, channels), jnp.float32),
            jax.ShapeDtypeStruct((rows // CHUNK * modes, channels), jnp.float32),
            jax.ShapeDtypeStruct((modes, channels), jnp.float32),
        ),
        in_specs=[
            rows_spec(blk, channels),
            whole_spec(hcol.shape),
            whole_spec(w_tab.shape),
            whole_spec(a8.shape),
        ],
        out_specs=(rows_spec(blk, channels), rows_spec(per, channels), whole_spec(a8.shape)),
        scratch_shapes=[pltpu.VMEM((modes, channels), jnp.float32)],
        compiler_params=sequential(),
    )(drive, hcol, w_tab, a8)


def gate(conv_local, query, sums, g_tab, a8, state_in, out_weight):
    rows, channels = conv_local.shape
    width = out_weight.shape[1]
    modes = a8.shape[0]
    blk = min(BLOCK, rows)
    per = blk // CHUNK * modes
    return pl.pallas_call(
        gate_kernel,
        grid=(rows // blk,),
        out_shape=jax.ShapeDtypeStruct((width, rows), jnp.bfloat16),
        in_specs=[
            rows_spec(blk, channels),
            rows_spec(blk, channels),
            rows_spec(per, channels),
            whole_spec(g_tab.shape),
            whole_spec(a8.shape),
            whole_spec(state_in.shape),
            whole_spec(out_weight.shape),
        ],
        out_specs=pl.BlockSpec((width, blk), lambda i: (0, i)),
        scratch_shapes=[
            pltpu.VMEM((modes, channels), jnp.float32),
            pltpu.VMEM((blk, channels), jnp.float32),
        ],
        compiler_params=sequential(),
    )(conv_local, query, sums, g_tab, a8, state_in, out_weight)


def per_device(tokens, in_weight, short_filter, mode_weight, decay_rate, out_weight):
    tok_rows = tokens.shape[0]
    channels = in_weight.shape[2]
    proj = jnp.einsum(
        "td,dkc->tkc",
        lax.all_gather(tokens, "tensor", axis=1, tiled=True),
        in_weight,
        preferred_element_type=jnp.float32,
    ).astype(jnp.bfloat16)
    rim = shifted(proj[tok_rows - (TAPS - 1) :], "context", 1)
    padded = jnp.concatenate([rim, proj], 0)
    filtered = jnp.zeros((tok_rows, 3, channels), jnp.float32)
    for tap_number in range(TAPS):
        begin = TAPS - 1 - tap_number
        filtered = filtered + short_filter[tap_number].astype(jnp.float32)[None] * padded[
            begin : begin + tok_rows
        ].astype(jnp.float32)
    query = filtered[:, 0]
    drive = filtered[:, 1] * filtered[:, 2]

    lam, g_tab, w_tab, hcol, a8 = chunk_tables(decay_rate, mode_weight)
    conv_local, sums, end_state = local_conv(drive, hcol, w_tab, a8)

    ends = lax.all_gather(end_state, "context", axis=0, tiled=False)
    block_count = ends.shape[0]
    me = lax.axis_index("context")
    gap = (me - 1 - jnp.arange(block_count)).astype(jnp.float32)
    factor = jnp.where(
        (gap >= 0.0)[:, None, None],
        jnp.exp(-lam[None] * (tok_rows * jnp.maximum(gap, 0.0))[:, None, None]),
        0.0,
    )
    state_in = jnp.sum(factor * ends, axis=0)

    partial_sums = gate(conv_local, query, sums, g_tab, a8, state_in, out_weight)
    summed = lax.psum_scatter(partial_sums, "tensor", scatter_dimension=0, tiled=True).T
    return summed


def solution(mesh):
    placed = (
        P(("groups", "context"), "tensor"),
        P(None, None, "tensor"),
        P(None, None, "tensor"),
        P("tensor", None),
        P("tensor", None),
        P("tensor", None),
    )
    return jax.shard_map(
        per_device,
        mesh=mesh,
        in_specs=placed,
        out_specs=P(("groups", "context"), "tensor"),
        check_vma=False,
    )
```

```python
import jax
import jax.numpy as jnp
from jax import lax
from jax.experimental import pallas as pl
from jax.experimental.pallas import tpu as pltpu
from jax.sharding import PartitionSpec as P

TAPS = 7
CHUNK = 8


def shifted(array, axis, by):
    size = lax.axis_size(axis)
    pairs = [(i, i + by) for i in range(size) if 0 <= i + by < size]
    return lax.ppermute(array, axis, pairs)


BLOCK = 512


def local_kernel(d_ref, hcol_ref, w_ref, a8_ref, conv_ref, sums_ref, end_ref, s_ref):
    rows = d_ref.shape[0]
    modes = a8_ref.shape[0]

    @pl.when(pl.program_id(0) == 0)
    def _():
        s_ref[...] = jnp.zeros(s_ref.shape, jnp.float32)

    def body(b, carry):
        start = pl.multiple_of(b * CHUNK, CHUNK)
        chunk = d_ref[pl.ds(start, CHUNK), :]
        acc = jnp.zeros(chunk.shape, jnp.float32)
        piece = jnp.zeros(s_ref.shape, jnp.float32)
        for j in range(CHUNK):
            row = chunk[j : j + 1, :]
            acc = acc + hcol_ref[j] * row
            piece = piece + w_ref[j] * row
        conv_ref[pl.ds(start, CHUNK), :] = acc
        sums_ref[pl.ds(pl.multiple_of(b * modes, modes), modes), :] = piece
        s_ref[...] = a8_ref[...] * s_ref[...] + piece
        return carry

    lax.fori_loop(0, rows // CHUNK, body, 0, unroll=4)
    end_ref[...] = s_ref[...]


def gate_kernel(conv_ref, q_ref, sums_ref, g_ref, a8_ref, sin_ref, wo_ref, out_ref, s_ref, gated_ref):
    rows = conv_ref.shape[0]
    modes = a8_ref.shape[0]

    @pl.when(pl.program_id(0) == 0)
    def _():
        s_ref[...] = sin_ref[...]

    def body(b, carry):
        start = pl.multiple_of(b * CHUNK, CHUNK)
        state = s_ref[...]
        acc = conv_ref[pl.ds(start, CHUNK), :]
        for n in range(modes):
            acc = acc + g_ref[n] * state[n : n + 1, :]
        gated_ref[pl.ds(start, CHUNK), :] = q_ref[pl.ds(start, CHUNK), :] * acc
        piece = sums_ref[pl.ds(pl.multiple_of(b * modes, modes), modes), :]
        s_ref[...] = a8_ref[...] * state + piece
        return carry

    lax.fori_loop(0, rows // CHUNK, body, 0, unroll=4)
    gated = gated_ref[...].astype(jnp.bfloat16)
    out_ref[...] = lax.dot_general(
        wo_ref[...], gated, (((0,), (1,)), ((), ())), preferred_element_type=jnp.float32
    ).astype(out_ref.dtype)


def rows_spec(rows, channels):
    return pl.BlockSpec((rows, channels), lambda i: (i, 0))


def whole_spec(shape):
    return pl.BlockSpec(shape, lambda i: (0,) * len(shape))


def sequential():
    return pltpu.CompilerParams(dimension_semantics=("arbitrary",))


def chunk_tables(decay_rate, mode_weight):
    lam = decay_rate.T
    amp = (mode_weight * jnp.sqrt(2.0 * decay_rate)).T
    steps = jnp.arange(CHUNK).astype(jnp.float32)
    g_tab = amp[:, None, :] * jnp.exp(-lam[:, None, :] * steps[None, :, None])
    w_tab = jnp.exp(-lam[None, :, :] * (CHUNK - steps)[:, None, None])
    h_short = jnp.sum(g_tab, axis=0)
    lag = steps[None, :] - steps[:, None]
    lag_index = jnp.clip(lag, 0, CHUNK - 1).astype(jnp.int32)
    hcol = jnp.where((lag >= 0)[:, :, None], h_short[lag_index], 0.0)
    a8 = jnp.exp(-lam * CHUNK)
    return lam, g_tab, w_tab, hcol, a8


def local_conv(drive, hcol, w_tab, a8):
    rows, channels = drive.shape
    modes = a8.shape[0]
    blk = min(BLOCK, rows)
    per = blk // CHUNK * modes
    return pl.pallas_call(
        local_kernel,
        grid=(rows // blk,),
        out_shape=(
            jax.ShapeDtypeStruct((rows, channels), jnp.float32),
            jax.ShapeDtypeStruct((rows // CHUNK * modes, channels), jnp.float32),
            jax.ShapeDtypeStruct((modes, channels), jnp.float32),
        ),
        in_specs=[
            rows_spec(blk, channels),
            whole_spec(hcol.shape),
            whole_spec(w_tab.shape),
            whole_spec(a8.shape),
        ],
        out_specs=(rows_spec(blk, channels), rows_spec(per, channels), whole_spec(a8.shape)),
        scratch_shapes=[pltpu.VMEM((modes, channels), jnp.float32)],
        compiler_params=sequential(),
    )(drive, hcol, w_tab, a8)


def gate(conv_local, query, sums, g_tab, a8, state_in, out_weight):
    rows, channels = conv_local.shape
    width = out_weight.shape[1]
    modes = a8.shape[0]
    blk = min(BLOCK, rows)
    per = blk // CHUNK * modes
    return pl.pallas_call(
        gate_kernel,
        grid=(rows // blk,),
        out_shape=jax.ShapeDtypeStruct((width, rows), jnp.bfloat16),
        in_specs=[
            rows_spec(blk, channels),
            rows_spec(blk, channels),
            rows_spec(per, channels),
            whole_spec(g_tab.shape),
            whole_spec(a8.shape),
            whole_spec(state_in.shape),
            whole_spec(out_weight.shape),
        ],
        out_specs=pl.BlockSpec((width, blk), lambda i: (0, i)),
        scratch_shapes=[
            pltpu.VMEM((modes, channels), jnp.float32),
            pltpu.VMEM((blk, channels), jnp.float32),
        ],
        compiler_params=sequential(),
    )(conv_local, query, sums, g_tab, a8, state_in, out_weight)


def per_device(tokens, in_weight, short_filter, mode_weight, decay_rate, out_weight):
    tok_rows = tokens.shape[0]
    channels = in_weight.shape[2]
    proj = jnp.einsum(
        "td,dkc->tkc",
        lax.all_gather(tokens, "tensor", axis=1, tiled=True),
        in_weight,
        preferred_element_type=jnp.float32,
    ).astype(jnp.bfloat16)
    rim = shifted(proj[tok_rows - (TAPS - 1) :], "context", 1)
    padded = jnp.concatenate([rim, proj], 0)
    filtered = jnp.zeros((tok_rows, 3, channels), jnp.float32)
    for tap_number in range(TAPS):
        begin = TAPS - 1 - tap_number
        filtered = filtered + short_filter[tap_number].astype(jnp.float32)[None] * padded[
            begin : begin + tok_rows
        ].astype(jnp.float32)
    query = filtered[:, 0]
    drive = filtered[:, 1] * filtered[:, 2]

    lam, g_tab, w_tab, hcol, a8 = chunk_tables(decay_rate, mode_weight)
    conv_local, sums, end_state = local_conv(drive, hcol, w_tab, a8)

    ends = lax.all_gather(end_state, "context", axis=0, tiled=False)
    block_count = ends.shape[0]
    me = lax.axis_index("context")
    gap = (me - 1 - jnp.arange(block_count)).astype(jnp.float32)
    factor = jnp.where(
        (gap >= 0.0)[:, None, None],
        jnp.exp(-lam[None] * (tok_rows * jnp.maximum(gap, 0.0))[:, None, None]),
        0.0,
    )
    state_in = jnp.sum(factor * ends, axis=0)

    partial_sums = gate(conv_local, query, sums, g_tab, a8, state_in, out_weight)
    summed = lax.psum_scatter(partial_sums, "tensor", scatter_dimension=0, tiled=True).T
    return summed


def solution(mesh):
    placed = (
        P(("groups", "context"), "tensor"),
        P(None, None, "tensor"),
        P(None, None, "tensor"),
        P("tensor", None),
        P("tensor", None),
        P("tensor", None),
    )
    return jax.shard_map(
        per_device,
        mesh=mesh,
        in_specs=placed,
        out_specs=P(("groups", "context"), "tensor"),
        check_vma=False,
    )
```

```python
import jax
import jax.numpy as jnp
from jax import lax
from jax.experimental import pallas as pl
from jax.experimental.pallas import tpu as pltpu
from jax.sharding import PartitionSpec as P

TAPS = 7
CHUNK = 8


def shifted(array, axis, by):
    size = lax.axis_size(axis)
    pairs = [(i, i + by) for i in range(size) if 0 <= i + by < size]
    return lax.ppermute(array, axis, pairs)


BLOCK = 256


def local_kernel(d_ref, hcol_ref, w_ref, a8_ref, conv_ref, sums_ref, end_ref, s_ref):
    rows = d_ref.shape[0]
    modes = a8_ref.shape[0]

    @pl.when(pl.program_id(0) == 0)
    def _():
        s_ref[...] = jnp.zeros(s_ref.shape, jnp.float32)

    def body(b, carry):
        start = pl.multiple_of(b * CHUNK, CHUNK)
        chunk = d_ref[pl.ds(start, CHUNK), :]
        acc = jnp.zeros(chunk.shape, jnp.float32)
        piece = jnp.zeros(s_ref.shape, jnp.float32)
        for j in range(CHUNK):
            row = chunk[j : j + 1, :]
            acc = acc + hcol_ref[j] * row
            piece = piece + w_ref[j] * row
        conv_ref[pl.ds(start, CHUNK), :] = acc
        sums_ref[pl.ds(pl.multiple_of(b * modes, modes), modes), :] = piece
        s_ref[...] = a8_ref[...] * s_ref[...] + piece
        return carry

    lax.fori_loop(0, rows // CHUNK, body, 0, unroll=4)
    end_ref[...] = s_ref[...]


def gate_kernel(conv_ref, q_ref, sums_ref, g_ref, a8_ref, sin_ref, wo_ref, out_ref, s_ref, gated_ref):
    rows = conv_ref.shape[0]
    modes = a8_ref.shape[0]

    @pl.when(pl.program_id(0) == 0)
    def _():
        s_ref[...] = sin_ref[...]

    def body(b, carry):
        start = pl.multiple_of(b * CHUNK, CHUNK)
        state = s_ref[...]
        acc = conv_ref[pl.ds(start, CHUNK), :]
        for n in range(modes):
            acc = acc + g_ref[n] * state[n : n + 1, :]
        gated_ref[pl.ds(start, CHUNK), :] = q_ref[pl.ds(start, CHUNK), :] * acc
        piece = sums_ref[pl.ds(pl.multiple_of(b * modes, modes), modes), :]
        s_ref[...] = a8_ref[...] * state + piece
        return carry

    lax.fori_loop(0, rows // CHUNK, body, 0, unroll=4)
    gated = gated_ref[...].astype(jnp.bfloat16)
    out_ref[...] = lax.dot_general(
        wo_ref[...], gated, (((0,), (1,)), ((), ())), preferred_element_type=jnp.float32
    ).astype(out_ref.dtype)


def rows_spec(rows, channels):
    return pl.BlockSpec((rows, channels), lambda i: (i, 0))


def whole_spec(shape):
    return pl.BlockSpec(shape, lambda i: (0,) * len(shape))


def sequential():
    return pltpu.CompilerParams(dimension_semantics=("arbitrary",))


def chunk_tables(decay_rate, mode_weight):
    lam = decay_rate.T
    amp = (mode_weight * jnp.sqrt(2.0 * decay_rate)).T
    steps = jnp.arange(CHUNK).astype(jnp.float32)
    g_tab = amp[:, None, :] * jnp.exp(-lam[:, None, :] * steps[None, :, None])
    w_tab = jnp.exp(-lam[None, :, :] * (CHUNK - steps)[:, None, None])
    h_short = jnp.sum(g_tab, axis=0)
    lag = steps[None, :] - steps[:, None]
    lag_index = jnp.clip(lag, 0, CHUNK - 1).astype(jnp.int32)
    hcol = jnp.where((lag >= 0)[:, :, None], h_short[lag_index], 0.0)
    a8 = jnp.exp(-lam * CHUNK)
    return lam, g_tab, w_tab, hcol, a8


def local_conv(drive, hcol, w_tab, a8):
    rows, channels = drive.shape
    modes = a8.shape[0]
    blk = min(BLOCK, rows)
    per = blk // CHUNK * modes
    return pl.pallas_call(
        local_kernel,
        grid=(rows // blk,),
        out_shape=(
            jax.ShapeDtypeStruct((rows, channels), jnp.float32),
            jax.ShapeDtypeStruct((rows // CHUNK * modes, channels), jnp.float32),
            jax.ShapeDtypeStruct((modes, channels), jnp.float32),
        ),
        in_specs=[
            rows_spec(blk, channels),
            whole_spec(hcol.shape),
            whole_spec(w_tab.shape),
            whole_spec(a8.shape),
        ],
        out_specs=(rows_spec(blk, channels), rows_spec(per, channels), whole_spec(a8.shape)),
        scratch_shapes=[pltpu.VMEM((modes, channels), jnp.float32)],
        compiler_params=sequential(),
    )(drive, hcol, w_tab, a8)


def gate(conv_local, query, sums, g_tab, a8, state_in, out_weight):
    rows, channels = conv_local.shape
    width = out_weight.shape[1]
    modes = a8.shape[0]
    blk = min(BLOCK, rows)
    per = blk // CHUNK * modes
    return pl.pallas_call(
        gate_kernel,
        grid=(rows // blk,),
        out_shape=jax.ShapeDtypeStruct((width, rows), jnp.bfloat16),
        in_specs=[
            rows_spec(blk, channels),
            rows_spec(blk, channels),
            rows_spec(per, channels),
            whole_spec(g_tab.shape),
            whole_spec(a8.shape),
            whole_spec(state_in.shape),
            whole_spec(out_weight.shape),
        ],
        out_specs=pl.BlockSpec((width, blk), lambda i: (0, i)),
        scratch_shapes=[
            pltpu.VMEM((modes, channels), jnp.float32),
            pltpu.VMEM((blk, channels), jnp.float32),
        ],
        compiler_params=sequential(),
    )(conv_local, query, sums, g_tab, a8, state_in, out_weight)


def per_device(tokens, in_weight, short_filter, mode_weight, decay_rate, out_weight):
    tok_rows = tokens.shape[0]
    channels = in_weight.shape[2]
    proj = jnp.einsum(
        "td,dkc->tkc",
        lax.all_gather(tokens, "tensor", axis=1, tiled=True),
        in_weight,
        preferred_element_type=jnp.float32,
    ).astype(jnp.bfloat16)
    rim = shifted(proj[tok_rows - (TAPS - 1) :], "context", 1)
    padded = jnp.concatenate([rim, proj], 0)
    filtered = jnp.zeros((tok_rows, 3, channels), jnp.float32)
    for tap_number in range(TAPS):
        begin = TAPS - 1 - tap_number
        filtered = filtered + short_filter[tap_number].astype(jnp.float32)[None] * padded[
            begin : begin + tok_rows
        ].astype(jnp.float32)
    query = filtered[:, 0]
    drive = filtered[:, 1] * filtered[:, 2]

    lam, g_tab, w_tab, hcol, a8 = chunk_tables(decay_rate, mode_weight)
    conv_local, sums, end_state = local_conv(drive, hcol, w_tab, a8)

    block_count = lax.axis_size("context")
    me = lax.axis_index("context")
    slots = jnp.zeros((block_count,) + end_state.shape, jnp.float32)
    slots = lax.dynamic_update_slice_in_dim(slots, end_state[None], me, 0)
    ends = lax.psum(slots, "context")
    gap = (me - 1 - jnp.arange(block_count)).astype(jnp.float32)
    factor = jnp.where(
        (gap >= 0.0)[:, None, None],
        jnp.exp(-lam[None] * (tok_rows * jnp.maximum(gap, 0.0))[:, None, None]),
        0.0,
    )
    state_in = jnp.sum(factor * ends, axis=0)

    partial_sums = gate(conv_local, query, sums, g_tab, a8, state_in, out_weight)
    summed = lax.psum_scatter(partial_sums, "tensor", scatter_dimension=0, tiled=True).T
    return summed


def solution(mesh):
    placed = (
        P(("groups", "context"), "tensor"),
        P(None, None, "tensor"),
        P(None, None, "tensor"),
        P("tensor", None),
        P("tensor", None),
        P("tensor", None),
    )
    return jax.shard_map(
        per_device,
        mesh=mesh,
        in_specs=placed,
        out_specs=P(("groups", "context"), "tensor"),
        check_vma=False,
    )
```

```python
import jax
import jax.numpy as jnp
from jax import lax
from jax.experimental import pallas as pl
from jax.experimental.pallas import tpu as pltpu
from jax.sharding import PartitionSpec as P

TAPS = 7
CHUNK = 8


def shifted(array, axis, by):
    size = lax.axis_size(axis)
    pairs = [(i, i + by) for i in range(size) if 0 <= i + by < size]
    return lax.ppermute(array, axis, pairs)


BLOCK = 256


def local_kernel(d_ref, hcol_ref, w_ref, a8_ref, conv_ref, sums_ref, end_ref, s_ref):
    rows = d_ref.shape[0]
    modes = a8_ref.shape[0]

    @pl.when(pl.program_id(0) == 0)
    def _():
        s_ref[...] = jnp.zeros(s_ref.shape, jnp.float32)

    def body(b, carry):
        start = pl.multiple_of(b * CHUNK, CHUNK)
        chunk = d_ref[pl.ds(start, CHUNK), :]
        acc = jnp.zeros(chunk.shape, jnp.float32)
        piece = jnp.zeros(s_ref.shape, jnp.float32)
        for j in range(CHUNK):
            row = chunk[j : j + 1, :]
            acc = acc + hcol_ref[j] * row
            piece = piece + w_ref[j] * row
        conv_ref[pl.ds(start, CHUNK), :] = acc
        sums_ref[pl.ds(pl.multiple_of(b * modes, modes), modes), :] = piece
        s_ref[...] = a8_ref[...] * s_ref[...] + piece
        return carry

    lax.fori_loop(0, rows // CHUNK, body, 0, unroll=4)
    end_ref[...] = s_ref[...]


def gate_kernel(conv_ref, q_ref, sums_ref, g_ref, a8_ref, sin_ref, wo_ref, out_ref, s_ref, gated_ref):
    rows = conv_ref.shape[0]
    modes = a8_ref.shape[0]

    @pl.when(pl.program_id(0) == 0)
    def _():
        s_ref[...] = sin_ref[...]

    def body(b, carry):
        start = pl.multiple_of(b * CHUNK, CHUNK)
        state = s_ref[...]
        acc = conv_ref[pl.ds(start, CHUNK), :]
        for n in range(modes):
            acc = acc + g_ref[n] * state[n : n + 1, :]
        gated_ref[pl.ds(start, CHUNK), :] = q_ref[pl.ds(start, CHUNK), :] * acc
        piece = sums_ref[pl.ds(pl.multiple_of(b * modes, modes), modes), :]
        s_ref[...] = a8_ref[...] * state + piece
        return carry

    lax.fori_loop(0, rows // CHUNK, body, 0, unroll=4)
    gated = gated_ref[...].astype(jnp.bfloat16)
    out_ref[...] = lax.dot_general(
        wo_ref[...], gated, (((0,), (1,)), ((), ())), preferred_element_type=jnp.float32
    ).astype(out_ref.dtype)


def rows_spec(rows, channels):
    return pl.BlockSpec((rows, channels), lambda i: (i, 0))


def whole_spec(shape):
    return pl.BlockSpec(shape, lambda i: (0,) * len(shape))


def sequential():
    return pltpu.CompilerParams(dimension_semantics=("arbitrary",))


def chunk_tables(decay_rate, mode_weight):
    lam = decay_rate.T
    amp = (mode_weight * jnp.sqrt(2.0 * decay_rate)).T
    steps = jnp.arange(CHUNK).astype(jnp.float32)
    g_tab = amp[:, None, :] * jnp.exp(-lam[:, None, :] * steps[None, :, None])
    w_tab = jnp.exp(-lam[None, :, :] * (CHUNK - steps)[:, None, None])
    h_short = jnp.sum(g_tab, axis=0)
    lag = steps[None, :] - steps[:, None]
    lag_index = jnp.clip(lag, 0, CHUNK - 1).astype(jnp.int32)
    hcol = jnp.where((lag >= 0)[:, :, None], h_short[lag_index], 0.0)
    a8 = jnp.exp(-lam * CHUNK)
    return lam, g_tab, w_tab, hcol, a8


def local_conv(planes, hcol, w_tab, a8):
    rows, channels = planes.shape[1:]
    modes = a8.shape[0]
    blk = min(BLOCK, rows)
    per = blk // CHUNK * modes
    return pl.pallas_call(
        local_kernel,
        grid=(rows // blk,),
        out_shape=(
            jax.ShapeDtypeStruct((rows, channels), jnp.float32),
            jax.ShapeDtypeStruct((rows // CHUNK * modes, channels), jnp.float32),
            jax.ShapeDtypeStruct((modes, channels), jnp.float32),
        ),
        in_specs=[
            pl.BlockSpec((None, blk, channels), lambda i: (1, i, 0)),
            whole_spec(hcol.shape),
            whole_spec(w_tab.shape),
            whole_spec(a8.shape),
        ],
        out_specs=(rows_spec(blk, channels), rows_spec(per, channels), whole_spec(a8.shape)),
        scratch_shapes=[pltpu.VMEM((modes, channels), jnp.float32)],
        compiler_params=sequential(),
    )(planes, hcol, w_tab, a8)


def gate(conv_local, query, sums, g_tab, a8, state_in, out_weight):
    rows, channels = conv_local.shape
    width = out_weight.shape[1]
    modes = a8.shape[0]
    blk = min(BLOCK, rows)
    per = blk // CHUNK * modes
    return pl.pallas_call(
        gate_kernel,
        grid=(rows // blk,),
        out_shape=jax.ShapeDtypeStruct((width, rows), jnp.bfloat16),
        in_specs=[
            rows_spec(blk, channels),
            pl.BlockSpec((None, blk, channels), lambda i: (0, i, 0)),
            rows_spec(per, channels),
            whole_spec(g_tab.shape),
            whole_spec(a8.shape),
            whole_spec(state_in.shape),
            whole_spec(out_weight.shape),
        ],
        out_specs=pl.BlockSpec((width, blk), lambda i: (0, i)),
        scratch_shapes=[
            pltpu.VMEM((modes, channels), jnp.float32),
            pltpu.VMEM((blk, channels), jnp.float32),
        ],
        compiler_params=sequential(),
    )(conv_local, query, sums, g_tab, a8, state_in, out_weight)


def per_device(tokens, in_weight, short_filter, mode_weight, decay_rate, out_weight):
    tok_rows = tokens.shape[0]
    channels = in_weight.shape[2]
    proj = jnp.einsum(
        "td,dkc->tkc",
        lax.all_gather(tokens, "tensor", axis=1, tiled=True),
        in_weight,
        preferred_element_type=jnp.float32,
    ).astype(jnp.bfloat16)
    rim = shifted(proj[tok_rows - (TAPS - 1) :], "context", 1)
    padded = jnp.concatenate([rim, proj], 0)
    filtered = jnp.zeros((tok_rows, 3, channels), jnp.float32)
    for tap_number in range(TAPS):
        begin = TAPS - 1 - tap_number
        filtered = filtered + short_filter[tap_number].astype(jnp.float32)[None] * padded[
            begin : begin + tok_rows
        ].astype(jnp.float32)
    planes = jnp.stack([filtered[:, 0], filtered[:, 1] * filtered[:, 2]], 0)

    lam, g_tab, w_tab, hcol, a8 = chunk_tables(decay_rate, mode_weight)
    conv_local, sums, end_state = local_conv(planes, hcol, w_tab, a8)

    ends = lax.all_gather(end_state, "context", axis=0, tiled=False)
    block_count = ends.shape[0]
    me = lax.axis_index("context")
    gap = (me - 1 - jnp.arange(block_count)).astype(jnp.float32)
    factor = jnp.where(
        (gap >= 0.0)[:, None, None],
        jnp.exp(-lam[None] * (tok_rows * jnp.maximum(gap, 0.0))[:, None, None]),
        0.0,
    )
    state_in = jnp.sum(factor * ends, axis=0)

    partial_sums = gate(conv_local, planes, sums, g_tab, a8, state_in, out_weight)
    summed = lax.psum_scatter(partial_sums, "tensor", scatter_dimension=0, tiled=True).T
    return summed


def solution(mesh):
    placed = (
        P(("groups", "context"), "tensor"),
        P(None, None, "tensor"),
        P(None, None, "tensor"),
        P("tensor", None),
        P("tensor", None),
        P("tensor", None),
    )
    return jax.shard_map(
        per_device,
        mesh=mesh,
        in_specs=placed,
        out_specs=P(("groups", "context"), "tensor"),
        check_vma=False,
    )
```

```python
import jax
import jax.numpy as jnp
from jax import lax
from jax.experimental import pallas as pl
from jax.experimental.pallas import tpu as pltpu
from jax.sharding import PartitionSpec as P

TAPS = 7
CHUNK = 8


def shifted(array, axis, by):
    size = lax.axis_size(axis)
    pairs = [(i, i + by) for i in range(size) if 0 <= i + by < size]
    return lax.ppermute(array, axis, pairs)


BLOCK = 256


def local_kernel(d_ref, hcol_ref, w_ref, a8_ref, conv_ref, sums_ref, end_ref, s_ref):
    rows = d_ref.shape[0]
    modes = a8_ref.shape[0]

    @pl.when(pl.program_id(0) == 0)
    def _():
        s_ref[...] = jnp.zeros(s_ref.shape, jnp.float32)

    def body(b, carry):
        start = pl.multiple_of(b * CHUNK, CHUNK)
        chunk = d_ref[pl.ds(start, CHUNK), :]
        acc = jnp.zeros(chunk.shape, jnp.float32)
        piece = jnp.zeros(s_ref.shape, jnp.float32)
        for j in range(CHUNK):
            row = chunk[j : j + 1, :]
            acc = acc + hcol_ref[j] * row
            piece = piece + w_ref[j] * row
        conv_ref[pl.ds(start, CHUNK), :] = acc
        sums_ref[pl.ds(pl.multiple_of(b * modes, modes), modes), :] = piece
        s_ref[...] = a8_ref[...] * s_ref[...] + piece
        return carry

    lax.fori_loop(0, rows // CHUNK, body, 0, unroll=4)
    end_ref[...] = s_ref[...]


def gate_kernel(conv_ref, q_ref, sums_ref, g_ref, a8_ref, sin_ref, wo_ref, out_ref, s_ref, gated_ref):
    rows = conv_ref.shape[0]
    modes = a8_ref.shape[0]

    @pl.when(pl.program_id(0) == 0)
    def _():
        s_ref[...] = sin_ref[...]

    def body(b, carry):
        start = pl.multiple_of(b * CHUNK, CHUNK)
        state = s_ref[...]
        acc = conv_ref[pl.ds(start, CHUNK), :]
        for n in range(modes):
            acc = acc + g_ref[n] * state[n : n + 1, :]
        gated_ref[pl.ds(start, CHUNK), :] = q_ref[pl.ds(start, CHUNK), :] * acc
        piece = sums_ref[pl.ds(pl.multiple_of(b * modes, modes), modes), :]
        s_ref[...] = a8_ref[...] * state + piece
        return carry

    lax.fori_loop(0, rows // CHUNK, body, 0, unroll=4)
    gated = gated_ref[...].astype(jnp.bfloat16)
    out_ref[...] = lax.dot_general(
        wo_ref[...], gated, (((0,), (1,)), ((), ())), preferred_element_type=jnp.float32
    ).astype(out_ref.dtype)


def rows_spec(rows, channels):
    return pl.BlockSpec((rows, channels), lambda i: (i, 0))


def whole_spec(shape):
    return pl.BlockSpec(shape, lambda i: (0,) * len(shape))


def sequential():
    return pltpu.CompilerParams(dimension_semantics=("arbitrary",))


def chunk_tables(decay_rate, mode_weight):
    lam = decay_rate.T
    amp = (mode_weight * jnp.sqrt(2.0 * decay_rate)).T
    steps = jnp.arange(CHUNK).astype(jnp.float32)
    g_tab = amp[:, None, :] * jnp.exp(-lam[:, None, :] * steps[None, :, None])
    w_tab = jnp.exp(-lam[None, :, :] * (CHUNK - steps)[:, None, None])
    h_short = jnp.sum(g_tab, axis=0)
    lag = steps[None, :] - steps[:, None]
    lag_index = jnp.clip(lag, 0, CHUNK - 1).astype(jnp.int32)
    hcol = jnp.where((lag >= 0)[:, :, None], h_short[lag_index], 0.0)
    a8 = jnp.exp(-lam * CHUNK)
    return lam, g_tab, w_tab, hcol, a8


def local_conv(drive, hcol, w_tab, a8):
    rows, channels = drive.shape
    modes = a8.shape[0]
    blk = min(BLOCK, rows)
    per = blk // CHUNK * modes
    return pl.pallas_call(
        local_kernel,
        grid=(rows // blk,),
        out_shape=(
            jax.ShapeDtypeStruct((rows, channels), jnp.float32),
            jax.ShapeDtypeStruct((rows // CHUNK * modes, channels), jnp.float32),
            jax.ShapeDtypeStruct((modes, channels), jnp.float32),
        ),
        in_specs=[
            rows_spec(blk, channels),
            whole_spec(hcol.shape),
            whole_spec(w_tab.shape),
            whole_spec(a8.shape),
        ],
        out_specs=(rows_spec(blk, channels), rows_spec(per, channels), whole_spec(a8.shape)),
        scratch_shapes=[pltpu.VMEM((modes, channels), jnp.float32)],
        compiler_params=sequential(),
    )(drive, hcol, w_tab, a8)


def gate(conv_local, query, sums, g_tab, a8, state_in, out_weight):
    rows, channels = conv_local.shape
    width = out_weight.shape[1]
    modes = a8.shape[0]
    blk = min(BLOCK, rows)
    per = blk // CHUNK * modes
    return pl.pallas_call(
        gate_kernel,
        grid=(rows // blk,),
        out_shape=jax.ShapeDtypeStruct((width, rows), jnp.bfloat16),
        in_specs=[
            rows_spec(blk, channels),
            rows_spec(blk, channels),
            rows_spec(per, channels),
            whole_spec(g_tab.shape),
            whole_spec(a8.shape),
            whole_spec(state_in.shape),
            whole_spec(out_weight.shape),
        ],
        out_specs=pl.BlockSpec((width, blk), lambda i: (0, i)),
        scratch_shapes=[
            pltpu.VMEM((modes, channels), jnp.float32),
            pltpu.VMEM((blk, channels), jnp.float32),
        ],
        compiler_params=sequential(),
    )(conv_local, query, sums, g_tab, a8, state_in, out_weight)


def per_device(tokens, in_weight, short_filter, mode_weight, decay_rate, out_weight):
    tok_rows = tokens.shape[0]
    channels = in_weight.shape[2]
    proj = jnp.einsum(
        "td,dkc->tkc",
        lax.all_gather(tokens, "tensor", axis=1, tiled=True),
        in_weight,
        preferred_element_type=jnp.float32,
    ).astype(jnp.bfloat16)
    rim_rows = TAPS - 1
    rim = shifted(proj[tok_rows - rim_rows :], "context", 1)
    taps = short_filter.astype(jnp.float32)
    padded = jnp.concatenate([jnp.zeros_like(rim), proj], 0)
    filtered = jnp.zeros((tok_rows, 3, channels), jnp.float32)
    for tap_number in range(TAPS):
        begin = rim_rows - tap_number
        filtered = filtered + taps[tap_number][None] * padded[begin : begin + tok_rows].astype(
            jnp.float32
        )
    edge = jnp.concatenate([rim, jnp.zeros_like(rim)], 0).astype(jnp.float32)
    fix = jnp.zeros((rim_rows, 3, channels), jnp.float32)
    for tap_number in range(1, TAPS):
        begin = rim_rows - tap_number
        fix = fix + taps[tap_number][None] * edge[begin : begin + rim_rows]
    filtered = filtered.at[:rim_rows].add(fix)
    query = filtered[:, 0]
    drive = filtered[:, 1] * filtered[:, 2]

    lam, g_tab, w_tab, hcol, a8 = chunk_tables(decay_rate, mode_weight)
    conv_local, sums, end_state = local_conv(drive, hcol, w_tab, a8)

    ends = lax.all_gather(end_state, "context", axis=0, tiled=False)
    block_count = ends.shape[0]
    me = lax.axis_index("context")
    gap = (me - 1 - jnp.arange(block_count)).astype(jnp.float32)
    factor = jnp.where(
        (gap >= 0.0)[:, None, None],
        jnp.exp(-lam[None] * (tok_rows * jnp.maximum(gap, 0.0))[:, None, None]),
        0.0,
    )
    state_in = jnp.sum(factor * ends, axis=0)

    partial_sums = gate(conv_local, query, sums, g_tab, a8, state_in, out_weight)
    summed = lax.psum_scatter(partial_sums, "tensor", scatter_dimension=0, tiled=True).T
    return summed


def solution(mesh):
    placed = (
        P(("groups", "context"), "tensor"),
        P(None, None, "tensor"),
        P(None, None, "tensor"),
        P("tensor", None),
        P("tensor", None),
        P("tensor", None),
    )
    return jax.shard_map(
        per_device,
        mesh=mesh,
        in_specs=placed,
        out_specs=P(("groups", "context"), "tensor"),
        check_vma=False,
    )
```

```python
import jax
import jax.numpy as jnp
from jax import lax
from jax.experimental import pallas as pl
from jax.experimental.pallas import tpu as pltpu
from jax.sharding import PartitionSpec as P

TAPS = 7
CHUNK = 8


def shifted(array, axis, by):
    size = lax.axis_size(axis)
    pairs = [(i, i + by) for i in range(size) if 0 <= i + by < size]
    return lax.ppermute(array, axis, pairs)


BLOCK = 256


def local_kernel(d_ref, hcol_ref, w_ref, a8_ref, conv_ref, sums_ref, end_ref, s_ref):
    rows = d_ref.shape[0]
    modes = a8_ref.shape[0]

    @pl.when(pl.program_id(0) == 0)
    def _():
        s_ref[...] = jnp.zeros(s_ref.shape, jnp.float32)

    def body(b, carry):
        start = pl.multiple_of(b * CHUNK, CHUNK)
        chunk = d_ref[pl.ds(start, CHUNK), :]
        acc = jnp.zeros(chunk.shape, jnp.float32)
        piece = jnp.zeros(s_ref.shape, jnp.float32)
        for j in range(CHUNK):
            row = chunk[j : j + 1, :]
            acc = acc + hcol_ref[j] * row
            piece = piece + w_ref[j] * row
        conv_ref[pl.ds(start, CHUNK), :] = acc
        sums_ref[pl.ds(pl.multiple_of(b * modes, modes), modes), :] = piece
        s_ref[...] = a8_ref[...] * s_ref[...] + piece
        return carry

    lax.fori_loop(0, rows // CHUNK, body, 0, unroll=4)
    end_ref[...] = s_ref[...]


def gate_kernel(conv_ref, q_ref, sums_ref, g_ref, a8_ref, sin_ref, wo_ref, out_ref, s_ref, gated_ref):
    rows = conv_ref.shape[0]
    modes = a8_ref.shape[0]

    @pl.when(pl.program_id(0) == 0)
    def _():
        s_ref[...] = sin_ref[...]

    def body(b, carry):
        start = pl.multiple_of(b * CHUNK, CHUNK)
        state = s_ref[...]
        acc = conv_ref[pl.ds(start, CHUNK), :]
        for n in range(modes):
            acc = acc + g_ref[n] * state[n : n + 1, :]
        gated_ref[pl.ds(start, CHUNK), :] = q_ref[pl.ds(start, CHUNK), :] * acc
        piece = sums_ref[pl.ds(pl.multiple_of(b * modes, modes), modes), :]
        s_ref[...] = a8_ref[...] * state + piece
        return carry

    lax.fori_loop(0, rows // CHUNK, body, 0, unroll=4)
    gated = gated_ref[...].astype(jnp.bfloat16)
    out_ref[...] = lax.dot_general(
        wo_ref[...], gated, (((1,), (1,)), ((), ())), preferred_element_type=jnp.float32
    ).astype(out_ref.dtype)


def rows_spec(rows, channels):
    return pl.BlockSpec((rows, channels), lambda i: (i, 0))


def whole_spec(shape):
    return pl.BlockSpec(shape, lambda i: (0,) * len(shape))


def sequential():
    return pltpu.CompilerParams(dimension_semantics=("arbitrary",))


def chunk_tables(decay_rate, mode_weight):
    lam = decay_rate.T
    amp = (mode_weight * jnp.sqrt(2.0 * decay_rate)).T
    steps = jnp.arange(CHUNK).astype(jnp.float32)
    g_tab = amp[:, None, :] * jnp.exp(-lam[:, None, :] * steps[None, :, None])
    w_tab = jnp.exp(-lam[None, :, :] * (CHUNK - steps)[:, None, None])
    h_short = jnp.sum(g_tab, axis=0)
    lag = steps[None, :] - steps[:, None]
    lag_index = jnp.clip(lag, 0, CHUNK - 1).astype(jnp.int32)
    hcol = jnp.where((lag >= 0)[:, :, None], h_short[lag_index], 0.0)
    a8 = jnp.exp(-lam * CHUNK)
    return lam, g_tab, w_tab, hcol, a8


def local_conv(drive, hcol, w_tab, a8):
    rows, channels = drive.shape
    modes = a8.shape[0]
    blk = min(BLOCK, rows)
    per = blk // CHUNK * modes
    return pl.pallas_call(
        local_kernel,
        grid=(rows // blk,),
        out_shape=(
            jax.ShapeDtypeStruct((rows, channels), jnp.float32),
            jax.ShapeDtypeStruct((rows // CHUNK * modes, channels), jnp.float32),
            jax.ShapeDtypeStruct((modes, channels), jnp.float32),
        ),
        in_specs=[
            rows_spec(blk, channels),
            whole_spec(hcol.shape),
            whole_spec(w_tab.shape),
            whole_spec(a8.shape),
        ],
        out_specs=(rows_spec(blk, channels), rows_spec(per, channels), whole_spec(a8.shape)),
        scratch_shapes=[pltpu.VMEM((modes, channels), jnp.float32)],
        compiler_params=sequential(),
    )(drive, hcol, w_tab, a8)


def gate(conv_local, query, sums, g_tab, a8, state_in, out_weight):
    rows, channels = conv_local.shape
    width = out_weight.shape[0]
    modes = a8.shape[0]
    blk = min(BLOCK, rows)
    per = blk // CHUNK * modes
    return pl.pallas_call(
        gate_kernel,
        grid=(rows // blk,),
        out_shape=jax.ShapeDtypeStruct((width, rows), jnp.bfloat16),
        in_specs=[
            rows_spec(blk, channels),
            rows_spec(blk, channels),
            rows_spec(per, channels),
            whole_spec(g_tab.shape),
            whole_spec(a8.shape),
            whole_spec(state_in.shape),
            whole_spec(out_weight.shape),
        ],
        out_specs=pl.BlockSpec((width, blk), lambda i: (0, i)),
        scratch_shapes=[
            pltpu.VMEM((modes, channels), jnp.float32),
            pltpu.VMEM((blk, channels), jnp.float32),
        ],
        compiler_params=sequential(),
    )(conv_local, query, sums, g_tab, a8, state_in, out_weight)


def per_device(tokens, in_weight, short_filter, mode_weight, decay_rate, out_weight):
    tok_rows = tokens.shape[0]
    channels = in_weight.shape[2]
    proj = jnp.einsum(
        "td,dkc->tkc",
        lax.all_gather(tokens, "tensor", axis=1, tiled=True),
        in_weight,
        preferred_element_type=jnp.float32,
    ).astype(jnp.bfloat16)
    rim = shifted(proj[tok_rows - (TAPS - 1) :], "context", 1)
    padded = jnp.concatenate([rim, proj], 0)
    filtered = jnp.zeros((tok_rows, 3, channels), jnp.float32)
    for tap_number in range(TAPS):
        begin = TAPS - 1 - tap_number
        filtered = filtered + short_filter[tap_number].astype(jnp.float32)[None] * padded[
            begin : begin + tok_rows
        ].astype(jnp.float32)
    query = filtered[:, 0]
    drive = filtered[:, 1] * filtered[:, 2]

    lam, g_tab, w_tab, hcol, a8 = chunk_tables(decay_rate, mode_weight)
    conv_local, sums, end_state = local_conv(drive, hcol, w_tab, a8)

    ends = lax.all_gather(end_state, "context", axis=0, tiled=False)
    block_count = ends.shape[0]
    me = lax.axis_index("context")
    gap = (me - 1 - jnp.arange(block_count)).astype(jnp.float32)
    factor = jnp.where(
        (gap >= 0.0)[:, None, None],
        jnp.exp(-lam[None] * (tok_rows * jnp.maximum(gap, 0.0))[:, None, None]),
        0.0,
    )
    state_in = jnp.sum(factor * ends, axis=0)

    partial_sums = gate(conv_local, query, sums, g_tab, a8, state_in, out_weight.T)
    summed = lax.psum_scatter(partial_sums, "tensor", scatter_dimension=0, tiled=True).T
    return summed


def solution(mesh):
    placed = (
        P(("groups", "context"), "tensor"),
        P(None, None, "tensor"),
        P(None, None, "tensor"),
        P("tensor", None),
        P("tensor", None),
        P("tensor", None),
    )
    return jax.shard_map(
        per_device,
        mesh=mesh,
        in_specs=placed,
        out_specs=P(("groups", "context"), "tensor"),
        check_vma=False,
    )
```

```python
import jax
import jax.numpy as jnp
from jax import lax
from jax.experimental import pallas as pl
from jax.experimental.pallas import tpu as pltpu
from jax.sharding import PartitionSpec as P

TAPS = 7
CHUNK = 8


def shifted(array, axis, by):
    size = lax.axis_size(axis)
    pairs = [(i, i + by) for i in range(size) if 0 <= i + by < size]
    return lax.ppermute(array, axis, pairs)


BLOCK = 256


def local_kernel(d_ref, hcol_ref, w_ref, a8_ref, conv_ref, sums_ref, end_ref, s_ref):
    rows = d_ref.shape[0]
    modes = a8_ref.shape[0]

    @pl.when(pl.program_id(0) == 0)
    def _():
        s_ref[...] = jnp.zeros(s_ref.shape, jnp.float32)

    def body(b, carry):
        start = pl.multiple_of(b * CHUNK, CHUNK)
        chunk = d_ref[pl.ds(start, CHUNK), :]
        acc = jnp.zeros(chunk.shape, jnp.float32)
        piece = jnp.zeros(s_ref.shape, jnp.float32)
        for j in range(CHUNK):
            row = chunk[j : j + 1, :]
            acc = acc + hcol_ref[j] * row
            piece = piece + w_ref[j] * row
        conv_ref[pl.ds(start, CHUNK), :] = acc
        sums_ref[pl.ds(pl.multiple_of(b * modes, modes), modes), :] = piece
        s_ref[...] = a8_ref[...] * s_ref[...] + piece
        return carry

    lax.fori_loop(0, rows // CHUNK, body, 0, unroll=4)
    end_ref[...] = s_ref[...]


def gate_kernel(conv_ref, q_ref, sums_ref, g_ref, a8_ref, sin_ref, wo_ref, out_ref, s_ref, gated_ref):
    rows = conv_ref.shape[0]
    modes = a8_ref.shape[0]

    @pl.when(pl.program_id(0) == 0)
    def _():
        s_ref[...] = sin_ref[...]

    def body(b, carry):
        start = pl.multiple_of(b * CHUNK, CHUNK)
        state = s_ref[...]
        acc = conv_ref[pl.ds(start, CHUNK), :]
        for n in range(modes):
            acc = acc + g_ref[n] * state[n : n + 1, :]
        gated_ref[pl.ds(start, CHUNK), :] = q_ref[pl.ds(start, CHUNK), :] * acc
        piece = sums_ref[pl.ds(pl.multiple_of(b * modes, modes), modes), :]
        s_ref[...] = a8_ref[...] * state + piece
        return carry

    lax.fori_loop(0, rows // CHUNK, body, 0, unroll=True)
    gated = gated_ref[...].astype(jnp.bfloat16)
    out_ref[...] = lax.dot_general(
        wo_ref[...], gated, (((0,), (1,)), ((), ())), preferred_element_type=jnp.float32
    ).astype(out_ref.dtype)


def rows_spec(rows, channels):
    return pl.BlockSpec((rows, channels), lambda i: (i, 0))


def whole_spec(shape):
    return pl.BlockSpec(shape, lambda i: (0,) * len(shape))


def sequential():
    return pltpu.CompilerParams(dimension_semantics=("arbitrary",))


def chunk_tables(decay_rate, mode_weight):
    lam = decay_rate.T
    amp = (mode_weight * jnp.sqrt(2.0 * decay_rate)).T
    steps = jnp.arange(CHUNK).astype(jnp.float32)
    g_tab = amp[:, None, :] * jnp.exp(-lam[:, None, :] * steps[None, :, None])
    w_tab = jnp.exp(-lam[None, :, :] * (CHUNK - steps)[:, None, None])
    h_short = jnp.sum(g_tab, axis=0)
    lag = steps[None, :] - steps[:, None]
    lag_index = jnp.clip(lag, 0, CHUNK - 1).astype(jnp.int32)
    hcol = jnp.where((lag >= 0)[:, :, None], h_short[lag_index], 0.0)
    a8 = jnp.exp(-lam * CHUNK)
    return lam, g_tab, w_tab, hcol, a8


def local_conv(drive, hcol, w_tab, a8):
    rows, channels = drive.shape
    modes = a8.shape[0]
    blk = min(BLOCK, rows)
    per = blk // CHUNK * modes
    return pl.pallas_call(
        local_kernel,
        grid=(rows // blk,),
        out_shape=(
            jax.ShapeDtypeStruct((rows, channels), jnp.float32),
            jax.ShapeDtypeStruct((rows // CHUNK * modes, channels), jnp.float32),
            jax.ShapeDtypeStruct((modes, channels), jnp.float32),
        ),
        in_specs=[
            rows_spec(blk, channels),
            whole_spec(hcol.shape),
            whole_spec(w_tab.shape),
            whole_spec(a8.shape),
        ],
        out_specs=(rows_spec(blk, channels), rows_spec(per, channels), whole_spec(a8.shape)),
        scratch_shapes=[pltpu.VMEM((modes, channels), jnp.float32)],
        compiler_params=sequential(),
    )(drive, hcol, w_tab, a8)


def gate(conv_local, query, sums, g_tab, a8, state_in, out_weight):
    rows, channels = conv_local.shape
    width = out_weight.shape[1]
    modes = a8.shape[0]
    blk = min(BLOCK, rows)
    per = blk // CHUNK * modes
    return pl.pallas_call(
        gate_kernel,
        grid=(rows // blk,),
        out_shape=jax.ShapeDtypeStruct((width, rows), jnp.bfloat16),
        in_specs=[
            rows_spec(blk, channels),
            rows_spec(blk, channels),
            rows_spec(per, channels),
            whole_spec(g_tab.shape),
            whole_spec(a8.shape),
            whole_spec(state_in.shape),
            whole_spec(out_weight.shape),
        ],
        out_specs=pl.BlockSpec((width, blk), lambda i: (0, i)),
        scratch_shapes=[
            pltpu.VMEM((modes, channels), jnp.float32),
            pltpu.VMEM((blk, channels), jnp.float32),
        ],
        compiler_params=sequential(),
    )(conv_local, query, sums, g_tab, a8, state_in, out_weight)


def per_device(tokens, in_weight, short_filter, mode_weight, decay_rate, out_weight):
    tok_rows = tokens.shape[0]
    channels = in_weight.shape[2]
    proj = jnp.einsum(
        "td,dkc->tkc",
        lax.all_gather(tokens, "tensor", axis=1, tiled=True),
        in_weight,
        preferred_element_type=jnp.float32,
    ).astype(jnp.bfloat16)
    rim = shifted(proj[tok_rows - (TAPS - 1) :], "context", 1)
    padded = jnp.concatenate([rim, proj], 0)
    filtered = jnp.zeros((tok_rows, 3, channels), jnp.float32)
    for tap_number in range(TAPS):
        begin = TAPS - 1 - tap_number
        filtered = filtered + short_filter[tap_number].astype(jnp.float32)[None] * padded[
            begin : begin + tok_rows
        ].astype(jnp.float32)
    query = filtered[:, 0]
    drive = filtered[:, 1] * filtered[:, 2]

    lam, g_tab, w_tab, hcol, a8 = chunk_tables(decay_rate, mode_weight)
    conv_local, sums, end_state = local_conv(drive, hcol, w_tab, a8)

    ends = lax.all_gather(end_state, "context", axis=0, tiled=False)
    block_count = ends.shape[0]
    me = lax.axis_index("context")
    gap = (me - 1 - jnp.arange(block_count)).astype(jnp.float32)
    factor = jnp.where(
        (gap >= 0.0)[:, None, None],
        jnp.exp(-lam[None] * (tok_rows * jnp.maximum(gap, 0.0))[:, None, None]),
        0.0,
    )
    state_in = jnp.sum(factor * ends, axis=0)

    partial_sums = gate(conv_local, query, sums, g_tab, a8, state_in, out_weight)
    summed = lax.psum_scatter(partial_sums, "tensor", scatter_dimension=0, tiled=True).T
    return summed


def solution(mesh):
    placed = (
        P(("groups", "context"), "tensor"),
        P(None, None, "tensor"),
        P(None, None, "tensor"),
        P("tensor", None),
        P("tensor", None),
        P("tensor", None),
    )
    return jax.shard_map(
        per_device,
        mesh=mesh,
        in_specs=placed,
        out_specs=P(("groups", "context"), "tensor"),
        check_vma=False,
    )
```

```python
import jax
import jax.numpy as jnp
from jax import lax
from jax.experimental import pallas as pl
from jax.experimental.pallas import tpu as pltpu
from jax.sharding import PartitionSpec as P

TAPS = 7
CHUNK = 8


def shifted(array, axis, by):
    size = lax.axis_size(axis)
    pairs = [(i, i + by) for i in range(size) if 0 <= i + by < size]
    return lax.ppermute(array, axis, pairs)


BLOCK = 256


def local_kernel(d_ref, hcol_ref, w_ref, a8_ref, conv_ref, sums_ref, end_ref, s_ref):
    rows = d_ref.shape[0]
    modes = a8_ref.shape[0]

    @pl.when(pl.program_id(0) == 0)
    def _():
        s_ref[...] = jnp.zeros(s_ref.shape, jnp.float32)

    def body(b, carry):
        start = pl.multiple_of(b * CHUNK, CHUNK)
        chunk = d_ref[pl.ds(start, CHUNK), :]
        acc = jnp.zeros(chunk.shape, jnp.float32)
        piece = jnp.zeros(s_ref.shape, jnp.float32)
        for j in range(CHUNK):
            row = chunk[j : j + 1, :]
            acc = acc + hcol_ref[j] * row
            piece = piece + w_ref[j] * row
        conv_ref[pl.ds(start, CHUNK), :] = acc
        sums_ref[pl.ds(pl.multiple_of(b * modes, modes), modes), :] = piece
        return a8_ref[...] * carry + piece

    s_ref[...] = lax.fori_loop(0, rows // CHUNK, body, s_ref[...], unroll=4)
    end_ref[...] = s_ref[...]


def gate_kernel(conv_ref, q_ref, sums_ref, g_ref, a8_ref, sin_ref, wo_ref, out_ref, s_ref, gated_ref):
    rows = conv_ref.shape[0]
    modes = a8_ref.shape[0]

    @pl.when(pl.program_id(0) == 0)
    def _():
        s_ref[...] = sin_ref[...]

    def body(b, state):
        start = pl.multiple_of(b * CHUNK, CHUNK)
        acc = conv_ref[pl.ds(start, CHUNK), :]
        for n in range(modes):
            acc = acc + g_ref[n] * state[n : n + 1, :]
        gated_ref[pl.ds(start, CHUNK), :] = q_ref[pl.ds(start, CHUNK), :] * acc
        piece = sums_ref[pl.ds(pl.multiple_of(b * modes, modes), modes), :]
        return a8_ref[...] * state + piece

    s_ref[...] = lax.fori_loop(0, rows // CHUNK, body, s_ref[...], unroll=4)
    gated = gated_ref[...].astype(jnp.bfloat16)
    out_ref[...] = lax.dot_general(
        wo_ref[...], gated, (((0,), (1,)), ((), ())), preferred_element_type=jnp.float32
    ).astype(out_ref.dtype)


def rows_spec(rows, channels):
    return pl.BlockSpec((rows, channels), lambda i: (i, 0))


def whole_spec(shape):
    return pl.BlockSpec(shape, lambda i: (0,) * len(shape))


def sequential():
    return pltpu.CompilerParams(dimension_semantics=("arbitrary",))


def chunk_tables(decay_rate, mode_weight):
    lam = decay_rate.T
    amp = (mode_weight * jnp.sqrt(2.0 * decay_rate)).T
    steps = jnp.arange(CHUNK).astype(jnp.float32)
    g_tab = amp[:, None, :] * jnp.exp(-lam[:, None, :] * steps[None, :, None])
    w_tab = jnp.exp(-lam[None, :, :] * (CHUNK - steps)[:, None, None])
    h_short = jnp.sum(g_tab, axis=0)
    lag = steps[None, :] - steps[:, None]
    lag_index = jnp.clip(lag, 0, CHUNK - 1).astype(jnp.int32)
    hcol = jnp.where((lag >= 0)[:, :, None], h_short[lag_index], 0.0)
    a8 = jnp.exp(-lam * CHUNK)
    return lam, g_tab, w_tab, hcol, a8


def local_conv(drive, hcol, w_tab, a8):
    rows, channels = drive.shape
    modes = a8.shape[0]
    blk = min(BLOCK, rows)
    per = blk // CHUNK * modes
    return pl.pallas_call(
        local_kernel,
        grid=(rows // blk,),
        out_shape=(
            jax.ShapeDtypeStruct((rows, channels), jnp.float32),
            jax.ShapeDtypeStruct((rows // CHUNK * modes, channels), jnp.float32),
            jax.ShapeDtypeStruct((modes, channels), jnp.float32),
        ),
        in_specs=[
            rows_spec(blk, channels),
            whole_spec(hcol.shape),
            whole_spec(w_tab.shape),
            whole_spec(a8.shape),
        ],
        out_specs=(rows_spec(blk, channels), rows_spec(per, channels), whole_spec(a8.shape)),
        scratch_shapes=[pltpu.VMEM((modes, channels), jnp.float32)],
        compiler_params=sequential(),
    )(drive, hcol, w_tab, a8)


def gate(conv_local, query, sums, g_tab, a8, state_in, out_weight):
    rows, channels = conv_local.shape
    width = out_weight.shape[1]
    modes = a8.shape[0]
    blk = min(BLOCK, rows)
    per = blk // CHUNK * modes
    return pl.pallas_call(
        gate_kernel,
        grid=(rows // blk,),
        out_shape=jax.ShapeDtypeStruct((width, rows), jnp.bfloat16),
        in_specs=[
            rows_spec(blk, channels),
            rows_spec(blk, channels),
            rows_spec(per, channels),
            whole_spec(g_tab.shape),
            whole_spec(a8.shape),
            whole_spec(state_in.shape),
            whole_spec(out_weight.shape),
        ],
        out_specs=pl.BlockSpec((width, blk), lambda i: (0, i)),
        scratch_shapes=[
            pltpu.VMEM((modes, channels), jnp.float32),
            pltpu.VMEM((blk, channels), jnp.float32),
        ],
        compiler_params=sequential(),
    )(conv_local, query, sums, g_tab, a8, state_in, out_weight)


def per_device(tokens, in_weight, short_filter, mode_weight, decay_rate, out_weight):
    tok_rows = tokens.shape[0]
    channels = in_weight.shape[2]
    proj = jnp.einsum(
        "td,dkc->tkc",
        lax.all_gather(tokens, "tensor", axis=1, tiled=True),
        in_weight,
        preferred_element_type=jnp.float32,
    ).astype(jnp.bfloat16)
    rim = shifted(proj[tok_rows - (TAPS - 1) :], "context", 1)
    padded = jnp.concatenate([rim, proj], 0)
    filtered = jnp.zeros((tok_rows, 3, channels), jnp.float32)
    for tap_number in range(TAPS):
        begin = TAPS - 1 - tap_number
        filtered = filtered + short_filter[tap_number].astype(jnp.float32)[None] * padded[
            begin : begin + tok_rows
        ].astype(jnp.float32)
    query = filtered[:, 0]
    drive = filtered[:, 1] * filtered[:, 2]

    lam, g_tab, w_tab, hcol, a8 = chunk_tables(decay_rate, mode_weight)
    conv_local, sums, end_state = local_conv(drive, hcol, w_tab, a8)

    ends = lax.all_gather(end_state, "context", axis=0, tiled=False)
    block_count = ends.shape[0]
    me = lax.axis_index("context")
    gap = (me - 1 - jnp.arange(block_count)).astype(jnp.float32)
    factor = jnp.where(
        (gap >= 0.0)[:, None, None],
        jnp.exp(-lam[None] * (tok_rows * jnp.maximum(gap, 0.0))[:, None, None]),
        0.0,
    )
    state_in = jnp.sum(factor * ends, axis=0)

    partial_sums = gate(conv_local, query, sums, g_tab, a8, state_in, out_weight)
    summed = lax.psum_scatter(partial_sums, "tensor", scatter_dimension=0, tiled=True).T
    return summed


def solution(mesh):
    placed = (
        P(("groups", "context"), "tensor"),
        P(None, None, "tensor"),
        P(None, None, "tensor"),
        P("tensor", None),
        P("tensor", None),
        P("tensor", None),
    )
    return jax.shard_map(
        per_device,
        mesh=mesh,
        in_specs=placed,
        out_specs=P(("groups", "context"), "tensor"),
        check_vma=False,
    )
```

```python
import jax
import jax.numpy as jnp
from jax import lax
from jax.experimental import pallas as pl
from jax.experimental.pallas import tpu as pltpu
from jax.sharding import PartitionSpec as P

TAPS = 7
CHUNK = 8


def shifted(array, axis, by):
    size = lax.axis_size(axis)
    pairs = [(i, i + by) for i in range(size) if 0 <= i + by < size]
    return lax.ppermute(array, axis, pairs)


BLOCK = 256


def local_kernel(d_ref, hcol_ref, w_ref, a8_ref, conv_ref, sums_ref, end_ref, s_ref):
    rows = d_ref.shape[0]
    modes = a8_ref.shape[0]

    @pl.when(pl.program_id(0) == 0)
    def _():
        s_ref[...] = jnp.zeros(s_ref.shape, jnp.float32)

    def body(b, carry):
        start = pl.multiple_of(b * CHUNK, CHUNK)
        chunk = d_ref[pl.ds(start, CHUNK), :]
        acc = jnp.zeros(chunk.shape, jnp.float32)
        piece = jnp.zeros(s_ref.shape, jnp.float32)
        for j in range(CHUNK):
            row = chunk[j : j + 1, :]
            acc = acc + hcol_ref[j] * row
            piece = piece + w_ref[j] * row
        conv_ref[pl.ds(start, CHUNK), :] = acc
        sums_ref[pl.ds(pl.multiple_of(b * modes, modes), modes), :] = piece
        s_ref[...] = a8_ref[...] * s_ref[...] + piece
        return carry

    lax.fori_loop(0, rows // CHUNK, body, 0, unroll=4)
    end_ref[...] = s_ref[...]


def gate_kernel(conv_ref, q_ref, sums_ref, g_ref, a8_ref, sin_ref, wo_ref, out_ref, s_ref, gated_ref):
    rows = conv_ref.shape[0]
    modes = a8_ref.shape[0]

    @pl.when(pl.program_id(0) == 0)
    def _():
        s_ref[...] = sin_ref[...]

    def body(b, carry):
        start = pl.multiple_of(b * CHUNK, CHUNK)
        state = s_ref[...]
        acc = conv_ref[pl.ds(start, CHUNK), :]
        for n in range(modes):
            acc = acc + g_ref[n] * state[n : n + 1, :]
        gated_ref[pl.ds(start, CHUNK), :] = q_ref[pl.ds(start, CHUNK), :] * acc
        piece = sums_ref[pl.ds(pl.multiple_of(b * modes, modes), modes), :]
        s_ref[...] = a8_ref[...] * state + piece
        return carry

    lax.fori_loop(0, rows // CHUNK, body, 0, unroll=4)
    gated = gated_ref[...].astype(jnp.bfloat16)
    out_ref[...] = lax.dot_general(
        wo_ref[...], gated, (((0,), (1,)), ((), ())), preferred_element_type=jnp.float32
    ).astype(out_ref.dtype)


def rows_spec(rows, channels):
    return pl.BlockSpec((rows, channels), lambda i: (i, 0))


def whole_spec(shape):
    return pl.BlockSpec(shape, lambda i: (0,) * len(shape))


def sequential():
    return pltpu.CompilerParams(dimension_semantics=("arbitrary",))


def chunk_tables(decay_rate, mode_weight):
    lam = decay_rate.T
    amp = (mode_weight * jnp.sqrt(2.0 * decay_rate)).T
    steps = jnp.arange(CHUNK).astype(jnp.float32)
    g_tab = amp[:, None, :] * jnp.exp(-lam[:, None, :] * steps[None, :, None])
    w_tab = jnp.exp(-lam[None, :, :] * (CHUNK - steps)[:, None, None])
    h_short = jnp.sum(g_tab, axis=0)
    lag = steps[None, :] - steps[:, None]
    lag_index = jnp.clip(lag, 0, CHUNK - 1).astype(jnp.int32)
    hcol = jnp.where((lag >= 0)[:, :, None], h_short[lag_index], 0.0)
    a8 = jnp.exp(-lam * CHUNK)
    return lam, g_tab, w_tab, hcol, a8


def local_conv(drive, hcol, w_tab, a8):
    rows, channels = drive.shape
    modes = a8.shape[0]
    blk = min(2 * BLOCK, rows)
    per = blk // CHUNK * modes
    return pl.pallas_call(
        local_kernel,
        grid=(rows // blk,),
        out_shape=(
            jax.ShapeDtypeStruct((rows, channels), jnp.float32),
            jax.ShapeDtypeStruct((rows // CHUNK * modes, channels), jnp.float32),
            jax.ShapeDtypeStruct((modes, channels), jnp.float32),
        ),
        in_specs=[
            rows_spec(blk, channels),
            whole_spec(hcol.shape),
            whole_spec(w_tab.shape),
            whole_spec(a8.shape),
        ],
        out_specs=(rows_spec(blk, channels), rows_spec(per, channels), whole_spec(a8.shape)),
        scratch_shapes=[pltpu.VMEM((modes, channels), jnp.float32)],
        compiler_params=sequential(),
    )(drive, hcol, w_tab, a8)


def gate(conv_local, query, sums, g_tab, a8, state_in, out_weight):
    rows, channels = conv_local.shape
    width = out_weight.shape[1]
    modes = a8.shape[0]
    blk = min(BLOCK, rows)
    per = blk // CHUNK * modes
    return pl.pallas_call(
        gate_kernel,
        grid=(rows // blk,),
        out_shape=jax.ShapeDtypeStruct((width, rows), jnp.bfloat16),
        in_specs=[
            rows_spec(blk, channels),
            rows_spec(blk, channels),
            rows_spec(per, channels),
            whole_spec(g_tab.shape),
            whole_spec(a8.shape),
            whole_spec(state_in.shape),
            whole_spec(out_weight.shape),
        ],
        out_specs=pl.BlockSpec((width, blk), lambda i: (0, i)),
        scratch_shapes=[
            pltpu.VMEM((modes, channels), jnp.float32),
            pltpu.VMEM((blk, channels), jnp.float32),
        ],
        compiler_params=sequential(),
    )(conv_local, query, sums, g_tab, a8, state_in, out_weight)


def per_device(tokens, in_weight, short_filter, mode_weight, decay_rate, out_weight):
    tok_rows = tokens.shape[0]
    channels = in_weight.shape[2]
    proj = jnp.einsum(
        "td,dkc->tkc",
        lax.all_gather(tokens, "tensor", axis=1, tiled=True),
        in_weight,
        preferred_element_type=jnp.float32,
    ).astype(jnp.bfloat16)
    rim = shifted(proj[tok_rows - (TAPS - 1) :], "context", 1)
    padded = jnp.concatenate([rim, proj], 0)
    filtered = jnp.zeros((tok_rows, 3, channels), jnp.float32)
    for tap_number in range(TAPS):
        begin = TAPS - 1 - tap_number
        filtered = filtered + short_filter[tap_number].astype(jnp.float32)[None] * padded[
            begin : begin + tok_rows
        ].astype(jnp.float32)
    query = filtered[:, 0]
    drive = filtered[:, 1] * filtered[:, 2]

    lam, g_tab, w_tab, hcol, a8 = chunk_tables(decay_rate, mode_weight)
    conv_local, sums, end_state = local_conv(drive, hcol, w_tab, a8)

    ends = lax.all_gather(end_state, "context", axis=0, tiled=False)
    block_count = ends.shape[0]
    me = lax.axis_index("context")
    gap = (me - 1 - jnp.arange(block_count)).astype(jnp.float32)
    factor = jnp.where(
        (gap >= 0.0)[:, None, None],
        jnp.exp(-lam[None] * (tok_rows * jnp.maximum(gap, 0.0))[:, None, None]),
        0.0,
    )
    state_in = jnp.sum(factor * ends, axis=0)

    partial_sums = gate(conv_local, query, sums, g_tab, a8, state_in, out_weight)
    summed = lax.psum_scatter(partial_sums, "tensor", scatter_dimension=0, tiled=True).T
    return summed


def solution(mesh):
    placed = (
        P(("groups", "context"), "tensor"),
        P(None, None, "tensor"),
        P(None, None, "tensor"),
        P("tensor", None),
        P("tensor", None),
        P("tensor", None),
    )
    return jax.shard_map(
        per_device,
        mesh=mesh,
        in_specs=placed,
        out_specs=P(("groups", "context"), "tensor"),
        check_vma=False,
    )
```
